32 devices in a mesh: grp: 4 (over z), mem: 8 (over y, x, core).
Axes of the slice: x: 2, y: 2, z: 4, core: 2. Of those that a mesh axis runs over, the one named last changes fastest.
Arguments:
- design: bfloat16 [8192, 1024], P(('grp', 'mem'))
- active_blocks: int32 [32, 8], P(('grp', 'mem')), may hold values from 0 to 31, as said below
- ridge: float32 [4096], replicated, may hold values from 0.5 to 2
Outputs:
- factored: float32 [8, 128, 128, 128], P('mem', 'grp')
The draws below stay inside these ranges and needn't reach their ends.
Inputs may be any that keep to these rules, and one draw needn't show every extreme that they name: active_blocks[d, a] % 8 == a for every device d and position a, so a device's blocks are distinct.
All inputs are finite; a program needn't handle non-finite values.
Results may differ from the reference program's by a relative error of at most 0.0003.
Values sent between devices are 32-bit elements; how exact they have to be, the bound alone decides.
No kernel may reach another device: no remote copies, remote signals or barrier semaphores. Data moves between devices by JAX's collectives and lax.ppermute only.
A program may use at most 64 MiB of HBM per device.

```python
import math
import jax
import jax.numpy as jnp
import numpy as np
from jax import lax

NB = 32
BLK = 128
ACT = 8
ROWS_DEV = 256
PANELS = 1
KCOEF = 4096
DEVS = 32
DIVISOR = 512
SLOTS = 128
N_MEM = 8


def draw_design(key, part):
    first, second, third = jax.random.split(key, 3)
    count = ROWS_DEV * DEVS
    noise = jax.random.normal(first, (count, ACT * BLK), jnp.float32)
    common = 0.5 * jax.random.normal(second, (count,), jnp.float32)
    scales = jnp.exp(jax.random.uniform(third, (count,), jnp.float32, jnp.log(0.2), jnp.log(2.0)))
    values = scales[:, None] * (noise + common[:, None])
    return values.astype(jnp.bfloat16)


def draw_active_blocks(key, part):
    picks = jax.random.randint(key, (DEVS, ACT), 0, NB // ACT)
    picks = picks.at[0].set(jnp.arange(ACT, dtype=jnp.int32) % (NB // ACT))
    return (jnp.arange(ACT, dtype=jnp.int32)[None, :] + ACT * picks).astype(jnp.int32)


def setup_inputs(seed: int = 0) -> dict:
    key_list = jax.random.split(jax.random.key(seed), 4)
    return {
        "design": draw_design(jax.random.fold_in(key_list[3], 71), 0),
        "active_blocks": draw_active_blocks(jax.random.fold_in(key_list[3], 71), 0),
        "ridge": jnp.clip(jnp.exp(jax.random.uniform(key_list[2], (KCOEF,), jnp.float32, math.log(0.5), math.log(2.0))), 0.5, 2.0),
    }


def panel_solve(column):
    count = column.shape[0]
    chol = jnp.linalg.cholesky(column[0])
    stacked = jnp.transpose(column, (2, 0, 1)).reshape(BLK, count * BLK)
    solved = lax.linalg.triangular_solve(chol, stacked, left_side=True, lower=True)
    lower_col = jnp.transpose(solved.reshape(BLK, count, BLK), (1, 2, 0))
    return lower_col.at[0].set(chol)

def reference(design, active_blocks, ridge):
    rows_all = design.reshape(DEVS, ROWS_DEV, ACT * BLK)

    def add_device(gram4, inputs):
        rows_dev, blocks = inputs
        wide = rows_dev.astype(jnp.float32)
        prod = jnp.dot(wide.T.astype(jnp.float32), wide.astype(jnp.float32), precision=lax.Precision.HIGHEST, preferred_element_type=jnp.float32)
        prod4 = jnp.transpose(prod.reshape(ACT, BLK, ACT, BLK), (0, 2, 1, 3))
        gram4 = gram4.at[blocks[:, None], :, blocks[None, :], :].add(prod4)
        return (gram4, None)
    start = jnp.zeros((NB, BLK, NB, BLK), jnp.float32)
    gram4, _ = lax.scan(add_device, start, (rows_all, active_blocks))
    matrix = gram4.reshape(KCOEF, KCOEF) / jnp.float32(DIVISOR) + jnp.diag(ridge)
    tiles = matrix.reshape(NB, BLK, NB, BLK)
    for step in range(PANELS):
        column = tiles[step:, :, step, :]
        lower_col = panel_solve(column)
        rest = lower_col[1:]
        update = jnp.einsum('ipr,jqr->ipjq', rest, rest, precision=lax.Precision.HIGHEST)
        tiles = tiles.at[step + 1:, :, step + 1:, :].add(-update)
        tiles = tiles.at[step:, :, step, :].set(lower_col)
        tiles = tiles.at[step, :, step + 1:, :].set(jnp.transpose(rest, (2, 0, 1)))
    classes = N_MEM // 8
    per_row = NB // 8
    owner = np.arange(N_MEM)[:, None]
    slot = np.arange(SLOTS)[None, :]
    row_ids = slot // per_row * classes + owner // 8
    col_ids = slot % per_row * 8 + owner % 8
    return tiles[row_ids, :, col_ids, :]
```

```python
import jax
import jax.numpy as jnp
from jax import lax
from jax.sharding import PartitionSpec as P

NB = 32
BLK = 128
ACT = 8
HI = lax.Precision.HIGHEST


def panel_solve(column):
    count = column.shape[0]
    chol = jnp.linalg.cholesky(column[0])
    stacked = jnp.transpose(column, (2, 0, 1)).reshape(BLK, count * BLK)
    solved = lax.linalg.triangular_solve(chol, stacked, left_side=True, lower=True)
    lower_col = jnp.transpose(solved.reshape(BLK, count, BLK), (1, 2, 0))
    return lower_col.at[0].set(chol)


def apply_step(tiles, lower_col, step, tile_rows, tile_cols):
    left_tiles = jnp.take(lower_col, jnp.maximum(tile_rows - step, 0), axis=0)
    right_tiles = jnp.take(lower_col, jnp.maximum(tile_cols - step, 0), axis=0)
    update = jnp.einsum("tpr,tqr->tpq", left_tiles, right_tiles, precision=HI)
    trailing = ((tile_rows > step) & (tile_cols > step))[:, None, None]
    on_column = ((tile_cols == step) & (tile_rows >= step))[:, None, None]
    on_row = ((tile_rows == step) & (tile_cols > step))[:, None, None]
    tiles = jnp.where(trailing, tiles - update, tiles)
    tiles = jnp.where(on_column, left_tiles, tiles)
    tiles = jnp.where(on_row, jnp.transpose(right_tiles, (0, 2, 1)), tiles)
    return tiles


def column_picker(step, tile_rows, tile_cols):
    wanted = step + jnp.arange(NB - step, dtype=jnp.int32)
    inside = (tile_cols == step) & (tile_rows >= step)
    return ((tile_rows[None, :] == wanted[:, None]) & inside[None, :]).astype(jnp.float32)


def on_device_general(design, active_blocks, ridge):
    n_mem = lax.axis_size("mem")
    n_grp = lax.axis_size("grp")
    member = lax.axis_index("mem")
    group = lax.axis_index("grp")
    classes = n_mem // 8
    per_pos = ACT // classes
    per_row = NB // ACT
    slot_count = NB // classes * per_row
    owned_count = slot_count // n_grp
    row_count = design.shape[0]
    residue = member // 8
    position = member % 8
    everyone = lax.all_gather(active_blocks, "mem", axis=0, tiled=True)
    blocks = design.reshape(row_count, ACT, BLK)
    left = blocks.reshape(row_count, per_pos, classes, BLK)
    outgoing = jnp.einsum("ncqk,nbl->qbckl", left, blocks, preferred_element_type=jnp.float32)
    outgoing = outgoing.reshape(n_mem, per_pos, BLK, BLK)
    received = lax.all_to_all(outgoing, "mem", split_axis=0, concat_axis=0, tiled=True)
    row_ids = jnp.take(everyone.reshape(n_mem, per_pos, classes), residue, axis=2)
    col_ids = jnp.take(everyone, position, axis=1)
    targets = row_ids // classes * per_row + (col_ids // 8)[:, None]
    onehot = (
        targets.reshape(-1)[None, :] == jnp.arange(slot_count, dtype=jnp.int32)[:, None]
    ).astype(jnp.float32)
    sums = jnp.dot(
        onehot,
        received.reshape(n_mem * per_pos, BLK * BLK),
        precision=HI,
        preferred_element_type=jnp.float32,
    )
    sums = sums.reshape(slot_count, BLK, BLK)
    owned = lax.psum_scatter(sums, "grp", scatter_dimension=0, tiled=True)
    slots = group * owned_count + jnp.arange(owned_count, dtype=jnp.int32)
    tile_rows = slots // per_row * classes + residue
    tile_cols = slots % per_row * 8 + position
    ridge_blocks = jnp.take(ridge.reshape(NB, BLK), tile_rows, axis=0)
    same = (tile_rows == tile_cols).astype(jnp.float32)
    extra = jnp.eye(BLK, dtype=jnp.float32)[None] * ridge_blocks[:, None, :] * same[:, None, None]
    divisor = jnp.float32(row_count * n_grp * n_mem // 16)
    tiles = owned / divisor + extra
    picker = column_picker(0, tile_rows, tile_cols)
    partial_value = jnp.einsum("it,tpq->ipq", picker, tiles, precision=HI)
    column = lax.psum(partial_value, ("grp", "mem"))
    lower_col = panel_solve(column)
    tiles = apply_step(tiles, lower_col, 0, tile_rows, tile_cols)
    return tiles[None]


def on_device_fast(design, active_blocks, ridge):
    n_mem = lax.axis_size("mem")
    n_grp = lax.axis_size("grp")
    member = lax.axis_index("mem")
    group = lax.axis_index("grp")
    per_row = NB // ACT
    row_count = design.shape[0]
    divisor = jnp.float32(row_count * n_grp * n_mem // 16)
    eye = jnp.eye(BLK, dtype=jnp.float32)
    ridge_blocks = ridge.reshape(NB, BLK)

    everyone = lax.all_gather(active_blocks, "mem", axis=0, tiled=True)
    blocks = design.reshape(row_count, ACT, BLK)
    outgoing = jnp.einsum("nak,nbl->bakl", blocks, blocks, preferred_element_type=jnp.float32)

    mine00 = jnp.where(active_blocks[0, 0] == 0, outgoing[0, 0], 0.0)
    gram00 = lax.psum(mine00, ("grp", "mem"))
    a00 = gram00 / divisor + eye * ridge_blocks[0][None, :]
    chol = jnp.linalg.cholesky(a00)
    chol_inv = lax.linalg.triangular_solve(chol, eye, left_side=True, lower=True)

    received = lax.all_to_all(outgoing, "mem", split_axis=0, concat_axis=0, tiled=True)
    received = received.reshape(n_mem, ACT, BLK, BLK)

    row_grp = everyone // 8
    col_grp = jnp.take(everyone, member, axis=1) // 8
    grp_ids = jnp.arange(n_grp, dtype=jnp.int32)
    q_ids = jnp.arange(per_row, dtype=jnp.int32)
    mask = (
        (row_grp[:, :, None, None] == grp_ids[None, None, :, None])
        & (col_grp[:, None, None, None] == q_ids[None, None, None, :])
    ).astype(jnp.float32)
    main = jnp.einsum("sagq,sakl->gaqkl", mask, received, precision=HI)
    main = main.reshape(n_grp, ACT * per_row, BLK, BLK)
    col_mask = (
        (col_grp[:, None] == grp_ids[None, :]) & (everyone[:, 0:1] == 0)
    ).astype(jnp.float32)
    col_part = jnp.einsum("sg,slk->gkl", col_mask, received[:, 0], precision=HI)
    send = jnp.concatenate([main, col_part[:, None]], axis=1)
    send = send.reshape(n_grp * (ACT * per_row + 1), BLK, BLK)
    got = lax.psum_scatter(send, "grp", scatter_dimension=0, tiled=True)
    owned = got[: ACT * per_row]
    col_tile = got[ACT * per_row] / divisor

    t = jnp.arange(ACT * per_row, dtype=jnp.int32)
    tile_rows = group * 8 + t // per_row
    tile_cols = (t % per_row) * 8 + member
    same = (tile_rows == tile_cols).astype(jnp.float32)
    diag = eye[None] * jnp.take(ridge_blocks, tile_rows, axis=0)[:, None, :] * same[:, None, None]
    tiles = owned / divisor + diag

    col_rows = lax.all_gather(col_tile, "mem", axis=0, tiled=False)
    col_cols = lax.all_gather(col_tile, "grp", axis=0, tiled=False)
    p_rows = jnp.einsum("ipr,qr->ipq", col_rows, chol_inv, precision=HI)
    p_cols = jnp.einsum("ipr,qr->ipq", col_cols, chol_inv, precision=HI)
    row_ids = group * 8 + jnp.arange(8, dtype=jnp.int32)
    col_ids = jnp.arange(per_row, dtype=jnp.int32) * 8 + member
    p_rows = jnp.where((row_ids == 0)[:, None, None], chol[None], p_rows)
    p_cols = jnp.where((col_ids == 0)[:, None, None], chol[None], p_cols)

    update = jnp.einsum("apr,qsr->aqps", p_rows, p_cols, precision=HI)
    update = update.reshape(ACT * per_row, BLK, BLK)
    left_tiles = jnp.repeat(p_rows, per_row, axis=0)
    right_tiles = jnp.tile(p_cols, (ACT, 1, 1))
    trailing = ((tile_rows > 0) & (tile_cols > 0))[:, None, None]
    on_column = (tile_cols == 0)[:, None, None]
    on_row = ((tile_rows == 0) & (tile_cols > 0))[:, None, None]
    tiles = jnp.where(trailing, tiles - update, tiles)
    tiles = jnp.where(on_column, left_tiles, tiles)
    tiles = jnp.where(on_row, jnp.transpose(right_tiles, (0, 2, 1)), tiles)
    return tiles[None]


def solution(mesh):
    n_mem = mesh.shape["mem"]
    n_grp = mesh.shape["grp"]
    fast = n_mem == 8 and n_grp * 8 == NB
    body = on_device_fast if fast else on_device_general
    in_specs = (P(("grp", "mem"), None), P(("grp", "mem"), None), P())
    out_specs = P("mem", "grp", None, None)
    return jax.shard_map(
        body, mesh=mesh, in_specs=in_specs, out_specs=out_specs, check_vma=False
    )
```

```python
import jax
import jax.numpy as jnp
from jax import lax
from jax.sharding import PartitionSpec as P

NB = 32
BLK = 128
ACT = 8
HI = lax.Precision.HIGHEST


def panel_solve(column):
    count = column.shape[0]
    chol = jnp.linalg.cholesky(column[0])
    stacked = jnp.transpose(column, (2, 0, 1)).reshape(BLK, count * BLK)
    solved = lax.linalg.triangular_solve(chol, stacked, left_side=True, lower=True)
    lower_col = jnp.transpose(solved.reshape(BLK, count, BLK), (1, 2, 0))
    return lower_col.at[0].set(chol)


def apply_step(tiles, lower_col, step, tile_rows, tile_cols):
    left_tiles = jnp.take(lower_col, jnp.maximum(tile_rows - step, 0), axis=0)
    right_tiles = jnp.take(lower_col, jnp.maximum(tile_cols - step, 0), axis=0)
    update = jnp.einsum("tpr,tqr->tpq", left_tiles, right_tiles, precision=HI)
    trailing = ((tile_rows > step) & (tile_cols > step))[:, None, None]
    on_column = ((tile_cols == step) & (tile_rows >= step))[:, None, None]
    on_row = ((tile_rows == step) & (tile_cols > step))[:, None, None]
    tiles = jnp.where(trailing, tiles - update, tiles)
    tiles = jnp.where(on_column, left_tiles, tiles)
    tiles = jnp.where(on_row, jnp.transpose(right_tiles, (0, 2, 1)), tiles)
    return tiles


def column_picker(step, tile_rows, tile_cols):
    wanted = step + jnp.arange(NB - step, dtype=jnp.int32)
    inside = (tile_cols == step) & (tile_rows >= step)
    return ((tile_rows[None, :] == wanted[:, None]) & inside[None, :]).astype(jnp.float32)


def on_device_general(design, active_blocks, ridge):
    n_mem = lax.axis_size("mem")
    n_grp = lax.axis_size("grp")
    member = lax.axis_index("mem")
    group = lax.axis_index("grp")
    classes = n_mem // 8
    per_pos = ACT // classes
    per_row = NB // ACT
    slot_count = NB // classes * per_row
    owned_count = slot_count // n_grp
    row_count = design.shape[0]
    residue = member // 8
    position = member % 8
    everyone = lax.all_gather(active_blocks, "mem", axis=0, tiled=True)
    blocks = design.reshape(row_count, ACT, BLK)
    left = blocks.reshape(row_count, per_pos, classes, BLK)
    outgoing = jnp.einsum("ncqk,nbl->qbckl", left, blocks, preferred_element_type=jnp.float32)
    outgoing = outgoing.reshape(n_mem, per_pos, BLK, BLK)
    received = lax.all_to_all(outgoing, "mem", split_axis=0, concat_axis=0, tiled=True)
    row_ids = jnp.take(everyone.reshape(n_mem, per_pos, classes), residue, axis=2)
    col_ids = jnp.take(everyone, position, axis=1)
    targets = row_ids // classes * per_row + (col_ids // 8)[:, None]
    onehot = (
        targets.reshape(-1)[None, :] == jnp.arange(slot_count, dtype=jnp.int32)[:, None]
    ).astype(jnp.float32)
    sums = jnp.dot(
        onehot,
        received.reshape(n_mem * per_pos, BLK * BLK),
        precision=HI,
        preferred_element_type=jnp.float32,
    )
    sums = sums.reshape(slot_count, BLK, BLK)
    owned = lax.psum_scatter(sums, "grp", scatter_dimension=0, tiled=True)
    slots = group * owned_count + jnp.arange(owned_count, dtype=jnp.int32)
    tile_rows = slots // per_row * classes + residue
    tile_cols = slots % per_row * 8 + position
    ridge_blocks = jnp.take(ridge.reshape(NB, BLK), tile_rows, axis=0)
    same = (tile_rows == tile_cols).astype(jnp.float32)
    extra = jnp.eye(BLK, dtype=jnp.float32)[None] * ridge_blocks[:, None, :] * same[:, None, None]
    divisor = jnp.float32(row_count * n_grp * n_mem // 16)
    tiles = owned / divisor + extra
    picker = column_picker(0, tile_rows, tile_cols)
    partial_value = jnp.einsum("it,tpq->ipq", picker, tiles, precision=HI)
    column = lax.psum(partial_value, ("grp", "mem"))
    lower_col = panel_solve(column)
    tiles = apply_step(tiles, lower_col, 0, tile_rows, tile_cols)
    return tiles[None]


def on_device_fast(design, active_blocks, ridge):
    n_mem = lax.axis_size("mem")
    n_grp = lax.axis_size("grp")
    member = lax.axis_index("mem")
    group = lax.axis_index("grp")
    per_row = NB // ACT
    chunks = 4
    per_chunk = ACT // chunks
    row_count = design.shape[0]
    divisor = jnp.float32(row_count * n_grp * n_mem // 16)
    eye = jnp.eye(BLK, dtype=jnp.float32)
    ridge_blocks = ridge.reshape(NB, BLK)

    everyone = lax.all_gather(active_blocks, "mem", axis=0, tiled=True)
    blocks = design.reshape(row_count, ACT, BLK)
    outgoing = jnp.einsum("nak,nbl->bakl", blocks, blocks, preferred_element_type=jnp.float32)

    row_grp = everyone // 8
    col_grp = jnp.take(everyone, member, axis=1) // 8
    zero_on = everyone[:, 0] == 0
    grp_ids = jnp.arange(n_grp, dtype=jnp.int32)
    q_ids = jnp.arange(per_row, dtype=jnp.int32)
    pos_ids = jnp.arange(per_chunk, dtype=jnp.int32)

    owned_parts = []
    prev = None
    for k in range(chunks):
        piece = outgoing[:, k * per_chunk:(k + 1) * per_chunk]
        if prev is not None:
            piece, prev = lax.optimization_barrier((piece, prev))
        got_piece = lax.all_to_all(piece, "mem", split_axis=0, concat_axis=0, tiled=True)
        got_piece = got_piece.reshape(n_mem, per_chunk, BLK, BLK)
        prev = got_piece
        rg = row_grp[:, k * per_chunk:(k + 1) * per_chunk]
        sel = (
            (pos_ids[None, :, None, None, None] == pos_ids[None, None, None, None, :])
            & (rg[None, None, None, :, :] == grp_ids[:, None, None, None, None])
            & (col_grp[None, None, None, :, None] == q_ids[None, None, :, None, None])
        )
        sel = sel.reshape(n_grp, per_chunk * per_row, n_mem * per_chunk)
        if k == 0:
            first = pos_ids == 0
            col_sel = (
                (col_grp[None, :, None] == grp_ids[:, None, None])
                & zero_on[None, :, None]
                & first[None, None, :]
            ).reshape(n_grp, 1, n_mem * per_chunk)
            a00_sel = (
                zero_on[None, :, None] & first[None, None, :] & (member == 0)
            ).reshape(1, 1, n_mem * per_chunk)
            a00_sel = jnp.broadcast_to(a00_sel, (n_grp, 1, n_mem * per_chunk))
            sel = jnp.concatenate([sel, col_sel, a00_sel], axis=1)
        width = sel.shape[1]
        send = jnp.dot(
            sel.reshape(n_grp * width, n_mem * per_chunk).astype(jnp.float32),
            got_piece.reshape(n_mem * per_chunk, BLK * BLK),
            precision=HI,
            preferred_element_type=jnp.float32,
        ).reshape(n_grp * width, BLK, BLK)
        got = lax.psum_scatter(send, "grp", scatter_dimension=0, tiled=True)
        owned_parts.append(got[: per_chunk * per_row])
        if k == 0:
            col_tile = jnp.transpose(got[per_chunk * per_row]) / divisor
            a00 = got[per_chunk * per_row + 1] / divisor + eye * ridge_blocks[0][None, :]
    owned = jnp.concatenate(owned_parts, axis=0)

    col_tile, a00, prev = lax.optimization_barrier((col_tile, a00, prev))
    pair = jnp.broadcast_to(jnp.stack([col_tile, a00])[None], (n_mem, 2, BLK, BLK))
    pairs = lax.all_to_all(pair, "mem", split_axis=0, concat_axis=0, tiled=True)
    col_rows = pairs[:, 0]
    a00 = pairs[0, 1]
    spread = jnp.broadcast_to(col_tile[None], (n_grp, BLK, BLK))
    col_cols = lax.all_to_all(spread, "grp", split_axis=0, concat_axis=0, tiled=True)
    chol = jnp.linalg.cholesky(a00)
    chol_inv = lax.linalg.triangular_solve(chol, eye, left_side=True, lower=True)

    t = jnp.arange(ACT * per_row, dtype=jnp.int32)
    tile_rows = group * 8 + t // per_row
    tile_cols = (t % per_row) * 8 + member
    same = (tile_rows == tile_cols).astype(jnp.float32)
    diag = eye[None] * jnp.take(ridge_blocks, tile_rows, axis=0)[:, None, :] * same[:, None, None]
    tiles = owned / divisor + diag

    p_rows = jnp.einsum("ipr,qr->ipq", col_rows, chol_inv, precision=HI)
    p_cols = jnp.einsum("ipr,qr->ipq", col_cols, chol_inv, precision=HI)
    row_ids = group * 8 + jnp.arange(8, dtype=jnp.int32)
    col_ids = jnp.arange(per_row, dtype=jnp.int32) * 8 + member
    p_rows = jnp.where((row_ids == 0)[:, None, None], chol[None], p_rows)
    p_cols = jnp.where((col_ids == 0)[:, None, None], chol[None], p_cols)

    update = jnp.einsum("apr,qsr->aqps", p_rows, p_cols, precision=HI)
    update = update.reshape(ACT * per_row, BLK, BLK)
    left_tiles = jnp.repeat(p_rows, per_row, axis=0)
    right_tiles = jnp.tile(p_cols, (ACT, 1, 1))
    trailing = ((tile_rows > 0) & (tile_cols > 0))[:, None, None]
    on_column = (tile_cols == 0)[:, None, None]
    on_row = ((tile_rows == 0) & (tile_cols > 0))[:, None, None]
    tiles = jnp.where(trailing, tiles - update, tiles)
    tiles = jnp.where(on_column, left_tiles, tiles)
    tiles = jnp.where(on_row, jnp.transpose(right_tiles, (0, 2, 1)), tiles)
    return tiles[None]


def solution(mesh):
    n_mem = mesh.shape["mem"]
    n_grp = mesh.shape["grp"]
    fast = n_mem == 8 and n_grp * 8 == NB
    body = on_device_fast if fast else on_device_general
    in_specs = (P(("grp", "mem"), None), P(("grp", "mem"), None), P())
    out_specs = P("mem", "grp", None, None)
    return jax.shard_map(
        body, mesh=mesh, in_specs=in_specs, out_specs=out_specs, check_vma=False
    )
```

```python
import jax
import jax.numpy as jnp
from jax import lax
from jax.sharding import PartitionSpec as P

NB = 32
BLK = 128
ACT = 8
HI = lax.Precision.HIGHEST


def panel_solve(column):
    count = column.shape[0]
    chol = jnp.linalg.cholesky(column[0])
    stacked = jnp.transpose(column, (2, 0, 1)).reshape(BLK, count * BLK)
    solved = lax.linalg.triangular_solve(chol, stacked, left_side=True, lower=True)
    lower_col = jnp.transpose(solved.reshape(BLK, count, BLK), (1, 2, 0))
    return lower_col.at[0].set(chol)


def apply_step(tiles, lower_col, step, tile_rows, tile_cols):
    left_tiles = jnp.take(lower_col, jnp.maximum(tile_rows - step, 0), axis=0)
    right_tiles = jnp.take(lower_col, jnp.maximum(tile_cols - step, 0), axis=0)
    update = jnp.einsum("tpr,tqr->tpq", left_tiles, right_tiles, precision=HI)
    trailing = ((tile_rows > step) & (tile_cols > step))[:, None, None]
    on_column = ((tile_cols == step) & (tile_rows >= step))[:, None, None]
    on_row = ((tile_rows == step) & (tile_cols > step))[:, None, None]
    tiles = jnp.where(trailing, tiles - update, tiles)
    tiles = jnp.where(on_column, left_tiles, tiles)
    tiles = jnp.where(on_row, jnp.transpose(right_tiles, (0, 2, 1)), tiles)
    return tiles


def column_picker(step, tile_rows, tile_cols):
    wanted = step + jnp.arange(NB - step, dtype=jnp.int32)
    inside = (tile_cols == step) & (tile_rows >= step)
    return ((tile_rows[None, :] == wanted[:, None]) & inside[None, :]).astype(jnp.float32)


def on_device_general(design, active_blocks, ridge):
    n_mem = lax.axis_size("mem")
    n_grp = lax.axis_size("grp")
    member = lax.axis_index("mem")
    group = lax.axis_index("grp")
    classes = n_mem // 8
    per_pos = ACT // classes
    per_row = NB // ACT
    slot_count = NB // classes * per_row
    owned_count = slot_count // n_grp
    row_count = design.shape[0]
    residue = member // 8
    position = member % 8
    everyone = lax.all_gather(active_blocks, "mem", axis=0, tiled=True)
    blocks = design.reshape(row_count, ACT, BLK)
    left = blocks.reshape(row_count, per_pos, classes, BLK)
    outgoing = jnp.einsum("ncqk,nbl->qbckl", left, blocks, preferred_element_type=jnp.float32)
    outgoing = outgoing.reshape(n_mem, per_pos, BLK, BLK)
    received = lax.all_to_all(outgoing, "mem", split_axis=0, concat_axis=0, tiled=True)
    row_ids = jnp.take(everyone.reshape(n_mem, per_pos, classes), residue, axis=2)
    col_ids = jnp.take(everyone, position, axis=1)
    targets = row_ids // classes * per_row + (col_ids // 8)[:, None]
    onehot = (
        targets.reshape(-1)[None, :] == jnp.arange(slot_count, dtype=jnp.int32)[:, None]
    ).astype(jnp.float32)
    sums = jnp.dot(
        onehot,
        received.reshape(n_mem * per_pos, BLK * BLK),
        precision=HI,
        preferred_element_type=jnp.float32,
    )
    sums = sums.reshape(slot_count, BLK, BLK)
    owned = lax.psum_scatter(sums, "grp", scatter_dimension=0, tiled=True)
    slots = group * owned_count + jnp.arange(owned_count, dtype=jnp.int32)
    tile_rows = slots // per_row * classes + residue
    tile_cols = slots % per_row * 8 + position
    ridge_blocks = jnp.take(ridge.reshape(NB, BLK), tile_rows, axis=0)
    same = (tile_rows == tile_cols).astype(jnp.float32)
    extra = jnp.eye(BLK, dtype=jnp.float32)[None] * ridge_blocks[:, None, :] * same[:, None, None]
    divisor = jnp.float32(row_count * n_grp * n_mem // 16)
    tiles = owned / divisor + extra
    picker = column_picker(0, tile_rows, tile_cols)
    partial_value = jnp.einsum("it,tpq->ipq", picker, tiles, precision=HI)
    column = lax.psum(partial_value, ("grp", "mem"))
    lower_col = panel_solve(column)
    tiles = apply_step(tiles, lower_col, 0, tile_rows, tile_cols)
    return tiles[None]


def on_device_fast(design, active_blocks, ridge):
    n_mem = lax.axis_size("mem")
    n_grp = lax.axis_size("grp")
    member = lax.axis_index("mem")
    group = lax.axis_index("grp")
    per_row = NB // ACT
    sizes = (1, 2, 2, 3)
    starts = (0, 1, 3, 5)
    row_count = design.shape[0]
    divisor = jnp.float32(row_count * n_grp * n_mem // 16)
    eye = jnp.eye(BLK, dtype=jnp.float32)
    ridge_blocks = ridge.reshape(NB, BLK)

    ids_out = jnp.broadcast_to(active_blocks[None], (n_mem, 1, ACT))
    everyone = lax.all_to_all(ids_out, "mem", split_axis=0, concat_axis=0, tiled=True)
    everyone = everyone.reshape(n_mem, ACT)
    blocks = design.reshape(row_count, ACT, BLK)
    outgoing = jnp.einsum("nak,nbl->bakl", blocks, blocks, preferred_element_type=jnp.float32)

    row_grp = everyone // 8
    col_grp = jnp.take(everyone, member, axis=1) // 8
    zero_on = everyone[:, 0] == 0
    grp_ids = jnp.arange(n_grp, dtype=jnp.int32)
    q_ids = jnp.arange(per_row, dtype=jnp.int32)

    owned_parts = []
    prev = None
    for k in range(len(sizes)):
        per_chunk = sizes[k]
        lo = starts[k]
        pos_ids = jnp.arange(per_chunk, dtype=jnp.int32)
        piece = outgoing[:, lo:lo + per_chunk]
        if prev is not None:
            piece, prev = lax.optimization_barrier((piece, prev))
        got_piece = lax.all_to_all(piece, "mem", split_axis=0, concat_axis=0, tiled=True)
        got_piece = got_piece.reshape(n_mem, per_chunk, BLK, BLK)
        prev = got_piece
        rg = row_grp[:, lo:lo + per_chunk]
        sel = (
            (pos_ids[None, :, None, None, None] == pos_ids[None, None, None, None, :])
            & (rg[None, None, None, :, :] == grp_ids[:, None, None, None, None])
            & (col_grp[None, None, None, :, None] == q_ids[None, None, :, None, None])
        )
        sel = sel.reshape(n_grp, per_chunk * per_row, n_mem * per_chunk)
        if k == 0:
            first = pos_ids == 0
            col_sel = (
                (col_grp[None, :, None] == grp_ids[:, None, None])
                & zero_on[None, :, None]
                & first[None, None, :]
            ).reshape(n_grp, 1, n_mem * per_chunk)
            sel = jnp.concatenate([sel, col_sel], axis=1)
        width = sel.shape[1]
        send = jnp.dot(
            sel.reshape(n_grp * width, n_mem * per_chunk).astype(jnp.float32),
            got_piece.reshape(n_mem * per_chunk, BLK * BLK),
            precision=HI,
            preferred_element_type=jnp.float32,
        ).reshape(n_grp * width, BLK, BLK)
        got = lax.psum_scatter(send, "grp", scatter_dimension=0, tiled=True)
        owned_parts.append(got[: per_chunk * per_row])
        if k == 0:
            col_tile = jnp.transpose(got[per_chunk * per_row]) / divisor
    owned = jnp.concatenate(owned_parts, axis=0)

    col_tile, prev = lax.optimization_barrier((col_tile, prev))
    spread = jnp.broadcast_to(col_tile[None], (n_grp, BLK, BLK))
    col_cols = lax.all_to_all(spread, "grp", split_axis=0, concat_axis=0, tiled=True)
    pair = jnp.broadcast_to(jnp.stack([col_tile, col_cols[0]])[None], (n_mem, 2, BLK, BLK))
    pairs = lax.all_to_all(pair, "mem", split_axis=0, concat_axis=0, tiled=True)
    col_rows = pairs[:, 0]
    a00 = pairs[0, 1] + eye * ridge_blocks[0][None, :]
    chol = jnp.linalg.cholesky(a00)
    chol_inv = lax.linalg.triangular_solve(chol, eye, left_side=True, lower=True)

    t = jnp.arange(ACT * per_row, dtype=jnp.int32)
    tile_rows = group * 8 + t // per_row
    tile_cols = (t % per_row) * 8 + member
    same = (tile_rows == tile_cols).astype(jnp.float32)
    diag = eye[None] * jnp.take(ridge_blocks, tile_rows, axis=0)[:, None, :] * same[:, None, None]
    tiles = owned / divisor + diag

    p_rows = jnp.einsum("ipr,qr->ipq", col_rows, chol_inv, precision=HI)
    p_cols = jnp.einsum("ipr,qr->ipq", col_cols, chol_inv, precision=HI)
    row_ids = group * 8 + jnp.arange(8, dtype=jnp.int32)
    col_ids = jnp.arange(per_row, dtype=jnp.int32) * 8 + member
    p_rows = jnp.where((row_ids == 0)[:, None, None], chol[None], p_rows)
    p_cols = jnp.where((col_ids == 0)[:, None, None], chol[None], p_cols)

    update = jnp.einsum("apr,qsr->aqps", p_rows, p_cols, precision=HI)
    update = update.reshape(ACT * per_row, BLK, BLK)
    left_tiles = jnp.repeat(p_rows, per_row, axis=0)
    right_tiles = jnp.tile(p_cols, (ACT, 1, 1))
    trailing = ((tile_rows > 0) & (tile_cols > 0))[:, None, None]
    on_column = (tile_cols == 0)[:, None, None]
    on_row = ((tile_rows == 0) & (tile_cols > 0))[:, None, None]
    tiles = jnp.where(trailing, tiles - update, tiles)
    tiles = jnp.where(on_column, left_tiles, tiles)
    tiles = jnp.where(on_row, jnp.transpose(right_tiles, (0, 2, 1)), tiles)
    return tiles[None]


def solution(mesh):
    n_mem = mesh.shape["mem"]
    n_grp = mesh.shape["grp"]
    fast = n_mem == 8 and n_grp * 8 == NB
    body = on_device_fast if fast else on_device_general
    in_specs = (P(("grp", "mem"), None), P(("grp", "mem"), None), P())
    out_specs = P("mem", "grp", None, None)
    return jax.shard_map(
        body, mesh=mesh, in_specs=in_specs, out_specs=out_specs, check_vma=False
    )
```

```python
import jax
import jax.numpy as jnp
from jax import lax
from jax.sharding import PartitionSpec as P

NB = 32
BLK = 128
ACT = 8
HI = lax.Precision.HIGHEST


def panel_solve(column):
    count = column.shape[0]
    chol = jnp.linalg.cholesky(column[0])
    stacked = jnp.transpose(column, (2, 0, 1)).reshape(BLK, count * BLK)
    solved = lax.linalg.triangular_solve(chol, stacked, left_side=True, lower=True)
    lower_col = jnp.transpose(solved.reshape(BLK, count, BLK), (1, 2, 0))
    return lower_col.at[0].set(chol)


def apply_step(tiles, lower_col, step, tile_rows, tile_cols):
    left_tiles = jnp.take(lower_col, jnp.maximum(tile_rows - step, 0), axis=0)
    right_tiles = jnp.take(lower_col, jnp.maximum(tile_cols - step, 0), axis=0)
    update = jnp.einsum("tpr,tqr->tpq", left_tiles, right_tiles, precision=HI)
    trailing = ((tile_rows > step) & (tile_cols > step))[:, None, None]
    on_column = ((tile_cols == step) & (tile_rows >= step))[:, None, None]
    on_row = ((tile_rows == step) & (tile_cols > step))[:, None, None]
    tiles = jnp.where(trailing, tiles - update, tiles)
    tiles = jnp.where(on_column, left_tiles, tiles)
    tiles = jnp.where(on_row, jnp.transpose(right_tiles, (0, 2, 1)), tiles)
    return tiles


def column_picker(step, tile_rows, tile_cols):
    wanted = step + jnp.arange(NB - step, dtype=jnp.int32)
    inside = (tile_cols == step) & (tile_rows >= step)
    return ((tile_rows[None, :] == wanted[:, None]) & inside[None, :]).astype(jnp.float32)


def on_device_general(design, active_blocks, ridge):
    n_mem = lax.axis_size("mem")
    n_grp = lax.axis_size("grp")
    member = lax.axis_index("mem")
    group = lax.axis_index("grp")
    classes = n_mem // 8
    per_pos = ACT // classes
    per_row = NB // ACT
    slot_count = NB // classes * per_row
    owned_count = slot_count // n_grp
    row_count = design.shape[0]
    residue = member // 8
    position = member % 8
    everyone = lax.all_gather(active_blocks, "mem", axis=0, tiled=True)
    blocks = design.reshape(row_count, ACT, BLK)
    left = blocks.reshape(row_count, per_pos, classes, BLK)
    outgoing = jnp.einsum("ncqk,nbl->qbckl", left, blocks, preferred_element_type=jnp.float32)
    outgoing = outgoing.reshape(n_mem, per_pos, BLK, BLK)
    received = lax.all_to_all(outgoing, "mem", split_axis=0, concat_axis=0, tiled=True)
    row_ids = jnp.take(everyone.reshape(n_mem, per_pos, classes), residue, axis=2)
    col_ids = jnp.take(everyone, position, axis=1)
    targets = row_ids // classes * per_row + (col_ids // 8)[:, None]
    onehot = (
        targets.reshape(-1)[None, :] == jnp.arange(slot_count, dtype=jnp.int32)[:, None]
    ).astype(jnp.float32)
    sums = jnp.dot(
        onehot,
        received.reshape(n_mem * per_pos, BLK * BLK),
        precision=HI,
        preferred_element_type=jnp.float32,
    )
    sums = sums.reshape(slot_count, BLK, BLK)
    owned = lax.psum_scatter(sums, "grp", scatter_dimension=0, tiled=True)
    slots = group * owned_count + jnp.arange(owned_count, dtype=jnp.int32)
    tile_rows = slots // per_row * classes + residue
    tile_cols = slots % per_row * 8 + position
    ridge_blocks = jnp.take(ridge.reshape(NB, BLK), tile_rows, axis=0)
    same = (tile_rows == tile_cols).astype(jnp.float32)
    extra = jnp.eye(BLK, dtype=jnp.float32)[None] * ridge_blocks[:, None, :] * same[:, None, None]
    divisor = jnp.float32(row_count * n_grp * n_mem // 16)
    tiles = owned / divisor + extra
    picker = column_picker(0, tile_rows, tile_cols)
    partial_value = jnp.einsum("it,tpq->ipq", picker, tiles, precision=HI)
    column = lax.psum(partial_value, ("grp", "mem"))
    lower_col = panel_solve(column)
    tiles = apply_step(tiles, lower_col, 0, tile_rows, tile_cols)
    return tiles[None]


def on_device_fast(design, active_blocks, ridge):
    n_mem = lax.axis_size("mem")
    n_grp = lax.axis_size("grp")
    member = lax.axis_index("mem")
    group = lax.axis_index("grp")
    per_row = NB // ACT
    sizes = (1, 2, 2, 3)
    starts = (0, 1, 3, 5)
    row_count = design.shape[0]
    divisor = jnp.float32(row_count * n_grp * n_mem // 16)
    eye = jnp.eye(BLK, dtype=jnp.float32)
    ridge_blocks = ridge.reshape(NB, BLK)

    blocks = design.reshape(row_count, ACT, BLK)
    id_rows = jnp.zeros((8, BLK), jnp.float32).at[0, :ACT].set(active_blocks[0].astype(jnp.float32))
    id_rows = jnp.broadcast_to(id_rows[None, None], (n_mem, 1, 8, BLK))
    grp_ids = jnp.arange(n_grp, dtype=jnp.int32)
    q_ids = jnp.arange(per_row, dtype=jnp.int32)

    owned_parts = []
    prev = None
    for k in range(len(sizes)):
        per_chunk = sizes[k]
        lo = starts[k]
        pos_ids = jnp.arange(per_chunk, dtype=jnp.int32)
        piece = jnp.einsum(
            "nak,nbl->bakl", blocks[:, lo:lo + per_chunk], blocks, preferred_element_type=jnp.float32
        )
        if prev is not None:
            piece, prev = lax.optimization_barrier((piece, prev))
        else:
            piece = jnp.concatenate([piece, id_rows], axis=2)
        got_piece = lax.all_to_all(piece, "mem", split_axis=0, concat_axis=0, tiled=True)
        if prev is None:
            everyone = got_piece[:, 0, BLK, :ACT].astype(jnp.int32)
            got_piece = got_piece[:, :, :BLK]
            row_grp = everyone // 8
            col_grp = jnp.take(everyone, member, axis=1) // 8
            zero_on = everyone[:, 0] == 0
        got_piece = got_piece.reshape(n_mem, per_chunk, BLK, BLK)
        prev = got_piece
        rg = row_grp[:, lo:lo + per_chunk]
        sel = (
            (pos_ids[None, :, None, None, None] == pos_ids[None, None, None, None, :])
            & (rg[None, None, None, :, :] == grp_ids[:, None, None, None, None])
            & (col_grp[None, None, None, :, None] == q_ids[None, None, :, None, None])
        )
        sel = sel.reshape(n_grp, per_chunk * per_row, n_mem * per_chunk)
        if k == 0:
            first = pos_ids == 0
            col_sel = (
                (col_grp[None, :, None] == grp_ids[:, None, None])
                & zero_on[None, :, None]
                & first[None, None, :]
            ).reshape(n_grp, 1, n_mem * per_chunk)
            sel = jnp.concatenate([sel, col_sel], axis=1)
        width = sel.shape[1]
        send = jnp.dot(
            sel.reshape(n_grp * width, n_mem * per_chunk).astype(jnp.float32),
            got_piece.reshape(n_mem * per_chunk, BLK * BLK),
            precision=HI,
            preferred_element_type=jnp.float32,
        ).reshape(n_grp * width, BLK, BLK)
        got = lax.psum_scatter(send, "grp", scatter_dimension=0, tiled=True)
        owned_parts.append(got[: per_chunk * per_row])
        if k == 0:
            col_tile = jnp.transpose(got[per_chunk * per_row]) / divisor
    owned = jnp.concatenate(owned_parts, axis=0)

    col_tile, prev = lax.optimization_barrier((col_tile, prev))
    spread = jnp.broadcast_to(col_tile[None], (n_grp, BLK, BLK))
    col_cols = lax.all_to_all(spread, "grp", split_axis=0, concat_axis=0, tiled=True)
    pair = jnp.broadcast_to(jnp.stack([col_tile, col_cols[0]])[None], (n_mem, 2, BLK, BLK))
    pairs = lax.all_to_all(pair, "mem", split_axis=0, concat_axis=0, tiled=True)
    col_rows = pairs[:, 0]
    a00 = pairs[0, 1] + eye * ridge_blocks[0][None, :]
    chol = jnp.linalg.cholesky(a00)
    chol_inv = lax.linalg.triangular_solve(chol, eye, left_side=True, lower=True)

    t = jnp.arange(ACT * per_row, dtype=jnp.int32)
    tile_rows = group * 8 + t // per_row
    tile_cols = (t % per_row) * 8 + member
    same = (tile_rows == tile_cols).astype(jnp.float32)
    diag = eye[None] * jnp.take(ridge_blocks, tile_rows, axis=0)[:, None, :] * same[:, None, None]
    tiles = owned / divisor + diag

    p_rows = jnp.einsum("ipr,qr->ipq", col_rows, chol_inv, precision=HI)
    p_cols = jnp.einsum("ipr,qr->ipq", col_cols, chol_inv, precision=HI)
    row_ids = group * 8 + jnp.arange(8, dtype=jnp.int32)
    col_ids = jnp.arange(per_row, dtype=jnp.int32) * 8 + member
    p_rows = jnp.where((row_ids == 0)[:, None, None], chol[None], p_rows)
    p_cols = jnp.where((col_ids == 0)[:, None, None], chol[None], p_cols)

    update = jnp.einsum("apr,qsr->aqps", p_rows, p_cols, precision=HI)
    update = update.reshape(ACT * per_row, BLK, BLK)
    left_tiles = jnp.repeat(p_rows, per_row, axis=0)
    right_tiles = jnp.tile(p_cols, (ACT, 1, 1))
    trailing = ((tile_rows > 0) & (tile_cols > 0))[:, None, None]
    on_column = (tile_cols == 0)[:, None, None]
    on_row = ((tile_rows == 0) & (tile_cols > 0))[:, None, None]
    tiles = jnp.where(trailing, tiles - update, tiles)
    tiles = jnp.where(on_column, left_tiles, tiles)
    tiles = jnp.where(on_row, jnp.transpose(right_tiles, (0, 2, 1)), tiles)
    return tiles[None]


def solution(mesh):
    n_mem = mesh.shape["mem"]
    n_grp = mesh.shape["grp"]
    fast = n_mem == 8 and n_grp * 8 == NB
    body = on_device_fast if fast else on_device_general
    in_specs = (P(("grp", "mem"), None), P(("grp", "mem"), None), P())
    out_specs = P("mem", "grp", None, None)
    return jax.shard_map(
        body, mesh=mesh, in_specs=in_specs, out_specs=out_specs, check_vma=False
    )
```

```python
import jax
import jax.numpy as jnp
from jax import lax
from jax.sharding import PartitionSpec as P

NB = 32
BLK = 128
ACT = 8
HI = lax.Precision.HIGHEST


def panel_solve(column):
    count = column.shape[0]
    chol = jnp.linalg.cholesky(column[0])
    stacked = jnp.transpose(column, (2, 0, 1)).reshape(BLK, count * BLK)
    solved = lax.linalg.triangular_solve(chol, stacked, left_side=True, lower=True)
    lower_col = jnp.transpose(solved.reshape(BLK, count, BLK), (1, 2, 0))
    return lower_col.at[0].set(chol)


def apply_step(tiles, lower_col, step, tile_rows, tile_cols):
    left_tiles = jnp.take(lower_col, jnp.maximum(tile_rows - step, 0), axis=0)
    right_tiles = jnp.take(lower_col, jnp.maximum(tile_cols - step, 0), axis=0)
    update = jnp.einsum("tpr,tqr->tpq", left_tiles, right_tiles, precision=HI)
    trailing = ((tile_rows > step) & (tile_cols > step))[:, None, None]
    on_column = ((tile_cols == step) & (tile_rows >= step))[:, None, None]
    on_row = ((tile_rows == step) & (tile_cols > step))[:, None, None]
    tiles = jnp.where(trailing, tiles - update, tiles)
    tiles = jnp.where(on_column, left_tiles, tiles)
    tiles = jnp.where(on_row, jnp.transpose(right_tiles, (0, 2, 1)), tiles)
    return tiles


def column_picker(step, tile_rows, tile_cols):
    wanted = step + jnp.arange(NB - step, dtype=jnp.int32)
    inside = (tile_cols == step) & (tile_rows >= step)
    return ((tile_rows[None, :] == wanted[:, None]) & inside[None, :]).astype(jnp.float32)


def on_device_general(design, active_blocks, ridge):
    n_mem = lax.axis_size("mem")
    n_grp = lax.axis_size("grp")
    member = lax.axis_index("mem")
    group = lax.axis_index("grp")
    classes = n_mem // 8
    per_pos = ACT // classes
    per_row = NB // ACT
    slot_count = NB // classes * per_row
    owned_count = slot_count // n_grp
    row_count = design.shape[0]
    residue = member // 8
    position = member % 8
    everyone = lax.all_gather(active_blocks, "mem", axis=0, tiled=True)
    blocks = design.reshape(row_count, ACT, BLK)
    left = blocks.reshape(row_count, per_pos, classes, BLK)
    outgoing = jnp.einsum("ncqk,nbl->qbckl", left, blocks, preferred_element_type=jnp.float32)
    outgoing = outgoing.reshape(n_mem, per_pos, BLK, BLK)
    received = lax.all_to_all(outgoing, "mem", split_axis=0, concat_axis=0, tiled=True)
    row_ids = jnp.take(everyone.reshape(n_mem, per_pos, classes), residue, axis=2)
    col_ids = jnp.take(everyone, position, axis=1)
    targets = row_ids // classes * per_row + (col_ids // 8)[:, None]
    onehot = (
        targets.reshape(-1)[None, :] == jnp.arange(slot_count, dtype=jnp.int32)[:, None]
    ).astype(jnp.float32)
    sums = jnp.dot(
        onehot,
        received.reshape(n_mem * per_pos, BLK * BLK),
        precision=HI,
        preferred_element_type=jnp.float32,
    )
    sums = sums.reshape(slot_count, BLK, BLK)
    owned = lax.psum_scatter(sums, "grp", scatter_dimension=0, tiled=True)
    slots = group * owned_count + jnp.arange(owned_count, dtype=jnp.int32)
    tile_rows = slots // per_row * classes + residue
    tile_cols = slots % per_row * 8 + position
    ridge_blocks = jnp.take(ridge.reshape(NB, BLK), tile_rows, axis=0)
    same = (tile_rows == tile_cols).astype(jnp.float32)
    extra = jnp.eye(BLK, dtype=jnp.float32)[None] * ridge_blocks[:, None, :] * same[:, None, None]
    divisor = jnp.float32(row_count * n_grp * n_mem // 16)
    tiles = owned / divisor + extra
    picker = column_picker(0, tile_rows, tile_cols)
    partial_value = jnp.einsum("it,tpq->ipq", picker, tiles, precision=HI)
    column = lax.psum(partial_value, ("grp", "mem"))
    lower_col = panel_solve(column)
    tiles = apply_step(tiles, lower_col, 0, tile_rows, tile_cols)
    return tiles[None]


def on_device_fast(design, active_blocks, ridge):
    n_mem = lax.axis_size("mem")
    n_grp = lax.axis_size("grp")
    member = lax.axis_index("mem")
    group = lax.axis_index("grp")
    per_row = NB // ACT
    sizes = (1, 2, 2, 3)
    starts = (0, 1, 3, 5)
    row_count = design.shape[0]
    divisor = jnp.float32(row_count * n_grp * n_mem // 16)
    eye = jnp.eye(BLK, dtype=jnp.float32)
    ridge_blocks = ridge.reshape(NB, BLK)

    blocks = design.reshape(row_count, ACT, BLK)
    id_rows = jnp.zeros((8, BLK), jnp.float32).at[0, :ACT].set(active_blocks[0].astype(jnp.float32))
    id_rows = jnp.broadcast_to(id_rows[None, None], (n_mem, 1, 8, BLK))
    grp_ids = jnp.arange(n_grp, dtype=jnp.int32)
    q_ids = jnp.arange(per_row, dtype=jnp.int32)

    owned_parts = []
    prev = None
    for k in range(len(sizes)):
        per_chunk = sizes[k]
        lo = starts[k]
        pos_ids = jnp.arange(per_chunk, dtype=jnp.int32)
        piece = jnp.einsum(
            "nak,nbl->bakl", blocks[:, lo:lo + per_chunk], blocks, preferred_element_type=jnp.float32
        )
        if prev is not None:
            piece, prev = lax.optimization_barrier((piece, prev))
        else:
            piece = jnp.concatenate([piece, id_rows], axis=2)
        got_piece = lax.all_to_all(piece, "mem", split_axis=0, concat_axis=0, tiled=True)
        if prev is None:
            everyone = got_piece[:, 0, BLK, :ACT].astype(jnp.int32)
            got_piece = got_piece[:, :, :BLK]
            row_grp = everyone // 8
            col_grp = jnp.take(everyone, member, axis=1) // 8
            zero_on = everyone[:, 0] == 0
        got_piece = got_piece.reshape(n_mem, per_chunk, BLK, BLK)
        prev = got_piece
        rg = row_grp[:, lo:lo + per_chunk]
        sel = (
            (pos_ids[None, :, None, None, None] == pos_ids[None, None, None, None, :])
            & (rg[None, None, None, :, :] == grp_ids[:, None, None, None, None])
            & (col_grp[None, None, None, :, None] == q_ids[None, None, :, None, None])
        )
        sel = sel.reshape(n_grp, per_chunk * per_row, n_mem * per_chunk)
        if k == 0:
            first = pos_ids == 0
            col_sel = (
                (col_grp[None, :, None] == grp_ids[:, None, None])
                & zero_on[None, :, None]
                & first[None, None, :]
            ).reshape(n_grp, 1, n_mem * per_chunk)
            sel = jnp.concatenate([sel, col_sel], axis=1)
        width = sel.shape[1]
        send = jnp.dot(
            sel.reshape(n_grp * width, n_mem * per_chunk).astype(jnp.float32),
            got_piece.reshape(n_mem * per_chunk, BLK * BLK),
            precision=HI,
            preferred_element_type=jnp.float32,
        ).reshape(n_grp * width, BLK, BLK)
        if k == len(sizes) - 1:
            parts = lax.all_to_all(
                send.reshape(n_grp, width, BLK, BLK), "grp", split_axis=0, concat_axis=0, tiled=True
            )
            got = jnp.sum(parts, axis=0)
        else:
            got = lax.psum_scatter(send, "grp", scatter_dimension=0, tiled=True)
        owned_parts.append(got[: per_chunk * per_row])
        if k == 0:
            col_tile = jnp.transpose(got[per_chunk * per_row]) / divisor
    owned = jnp.concatenate(owned_parts, axis=0)

    col_tile, prev = lax.optimization_barrier((col_tile, prev))
    spread = jnp.broadcast_to(col_tile[None], (n_grp, BLK, BLK))
    col_cols = lax.all_to_all(spread, "grp", split_axis=0, concat_axis=0, tiled=True)
    pair = jnp.broadcast_to(jnp.stack([col_tile, col_cols[0]])[None], (n_mem, 2, BLK, BLK))
    pairs = lax.all_to_all(pair, "mem", split_axis=0, concat_axis=0, tiled=True)
    col_rows = pairs[:, 0]
    a00 = pairs[0, 1] + eye * ridge_blocks[0][None, :]
    chol = jnp.linalg.cholesky(a00)
    chol_inv = lax.linalg.triangular_solve(chol, eye, left_side=True, lower=True)

    t = jnp.arange(ACT * per_row, dtype=jnp.int32)
    tile_rows = group * 8 + t // per_row
    tile_cols = (t % per_row) * 8 + member
    same = (tile_rows == tile_cols).astype(jnp.float32)
    diag = eye[None] * jnp.take(ridge_blocks, tile_rows, axis=0)[:, None, :] * same[:, None, None]
    tiles = owned / divisor + diag

    p_rows = jnp.einsum("ipr,qr->ipq", col_rows, chol_inv, precision=HI)
    p_cols = jnp.einsum("ipr,qr->ipq", col_cols, chol_inv, precision=HI)
    row_ids = group * 8 + jnp.arange(8, dtype=jnp.int32)
    col_ids = jnp.arange(per_row, dtype=jnp.int32) * 8 + member
    p_rows = jnp.where((row_ids == 0)[:, None, None], chol[None], p_rows)
    p_cols = jnp.where((col_ids == 0)[:, None, None], chol[None], p_cols)

    update = jnp.einsum("apr,qsr->aqps", p_rows, p_cols, precision=HI)
    update = update.reshape(ACT * per_row, BLK, BLK)
    left_tiles = jnp.repeat(p_rows, per_row, axis=0)
    right_tiles = jnp.tile(p_cols, (ACT, 1, 1))
    trailing = ((tile_rows > 0) & (tile_cols > 0))[:, None, None]
    on_column = (tile_cols == 0)[:, None, None]
    on_row = ((tile_rows == 0) & (tile_cols > 0))[:, None, None]
    tiles = jnp.where(trailing, tiles - update, tiles)
    tiles = jnp.where(on_column, left_tiles, tiles)
    tiles = jnp.where(on_row, jnp.transpose(right_tiles, (0, 2, 1)), tiles)
    return tiles[None]


def solution(mesh):
    n_mem = mesh.shape["mem"]
    n_grp = mesh.shape["grp"]
    fast = n_mem == 8 and n_grp * 8 == NB
    body = on_device_fast if fast else on_device_general
    in_specs = (P(("grp", "mem"), None), P(("grp", "mem"), None), P())
    out_specs = P("mem", "grp", None, None)
    return jax.shard_map(
        body, mesh=mesh, in_specs=in_specs, out_specs=out_specs, check_vma=False
    )
```

```python
import jax
import jax.numpy as jnp
from jax import lax
from jax.sharding import PartitionSpec as P

NB = 32
BLK = 128
ACT = 8
HI = lax.Precision.HIGHEST


def panel_solve(column):
    count = column.shape[0]
    chol = jnp.linalg.cholesky(column[0])
    stacked = jnp.transpose(column, (2, 0, 1)).reshape(BLK, count * BLK)
    solved = lax.linalg.triangular_solve(chol, stacked, left_side=True, lower=True)
    lower_col = jnp.transpose(solved.reshape(BLK, count, BLK), (1, 2, 0))
    return lower_col.at[0].set(chol)


def apply_step(tiles, lower_col, step, tile_rows, tile_cols):
    left_tiles = jnp.take(lower_col, jnp.maximum(tile_rows - step, 0), axis=0)
    right_tiles = jnp.take(lower_col, jnp.maximum(tile_cols - step, 0), axis=0)
    update = jnp.einsum("tpr,tqr->tpq", left_tiles, right_tiles, precision=HI)
    trailing = ((tile_rows > step) & (tile_cols > step))[:, None, None]
    on_column = ((tile_cols == step) & (tile_rows >= step))[:, None, None]
    on_row = ((tile_rows == step) & (tile_cols > step))[:, None, None]
    tiles = jnp.where(trailing, tiles - update, tiles)
    tiles = jnp.where(on_column, left_tiles, tiles)
    tiles = jnp.where(on_row, jnp.transpose(right_tiles, (0, 2, 1)), tiles)
    return tiles


def column_picker(step, tile_rows, tile_cols):
    wanted = step + jnp.arange(NB - step, dtype=jnp.int32)
    inside = (tile_cols == step) & (tile_rows >= step)
    return ((tile_rows[None, :] == wanted[:, None]) & inside[None, :]).astype(jnp.float32)


def on_device_general(design, active_blocks, ridge):
    n_mem = lax.axis_size("mem")
    n_grp = lax.axis_size("grp")
    member = lax.axis_index("mem")
    group = lax.axis_index("grp")
    classes = n_mem // 8
    per_pos = ACT // classes
    per_row = NB // ACT
    slot_count = NB // classes * per_row
    owned_count = slot_count // n_grp
    row_count = design.shape[0]
    residue = member // 8
    position = member % 8
    everyone = lax.all_gather(active_blocks, "mem", axis=0, tiled=True)
    blocks = design.reshape(row_count, ACT, BLK)
    left = blocks.reshape(row_count, per_pos, classes, BLK)
    outgoing = jnp.einsum("ncqk,nbl->qbckl", left, blocks, preferred_element_type=jnp.float32)
    outgoing = outgoing.reshape(n_mem, per_pos, BLK, BLK)
    received = lax.all_to_all(outgoing, "mem", split_axis=0, concat_axis=0, tiled=True)
    row_ids = jnp.take(everyone.reshape(n_mem, per_pos, classes), residue, axis=2)
    col_ids = jnp.take(everyone, position, axis=1)
    targets = row_ids // classes * per_row + (col_ids // 8)[:, None]
    onehot = (
        targets.reshape(-1)[None, :] == jnp.arange(slot_count, dtype=jnp.int32)[:, None]
    ).astype(jnp.float32)
    sums = jnp.dot(
        onehot,
        received.reshape(n_mem * per_pos, BLK * BLK),
        precision=HI,
        preferred_element_type=jnp.float32,
    )
    sums = sums.reshape(slot_count, BLK, BLK)
    owned = lax.psum_scatter(sums, "grp", scatter_dimension=0, tiled=True)
    slots = group * owned_count + jnp.arange(owned_count, dtype=jnp.int32)
    tile_rows = slots // per_row * classes + residue
    tile_cols = slots % per_row * 8 + position
    ridge_blocks = jnp.take(ridge.reshape(NB, BLK), tile_rows, axis=0)
    same = (tile_rows == tile_cols).astype(jnp.float32)
    extra = jnp.eye(BLK, dtype=jnp.float32)[None] * ridge_blocks[:, None, :] * same[:, None, None]
    divisor = jnp.float32(row_count * n_grp * n_mem // 16)
    tiles = owned / divisor + extra
    picker = column_picker(0, tile_rows, tile_cols)
    partial_value = jnp.einsum("it,tpq->ipq", picker, tiles, precision=HI)
    column = lax.psum(partial_value, ("grp", "mem"))
    lower_col = panel_solve(column)
    tiles = apply_step(tiles, lower_col, 0, tile_rows, tile_cols)
    return tiles[None]


def on_device_fast(design, active_blocks, ridge):
    n_mem = lax.axis_size("mem")
    n_grp = lax.axis_size("grp")
    member = lax.axis_index("mem")
    group = lax.axis_index("grp")
    per_row = NB // ACT
    sizes = (1, 2, 2, 3)
    starts = (0, 1, 3, 5)
    tail = starts[-1]
    row_count = design.shape[0]
    divisor = jnp.float32(row_count * n_grp * n_mem // 16)
    eye = jnp.eye(BLK, dtype=jnp.float32)
    ridge_blocks = ridge.reshape(NB, BLK)

    blocks = design.reshape(row_count, ACT, BLK)
    id_rows = jnp.zeros((8, BLK), jnp.float32).at[0, :ACT].set(active_blocks[0].astype(jnp.float32))
    id_rows = jnp.broadcast_to(id_rows[None, None], (n_mem, 2, 8, BLK))
    grp_ids = jnp.arange(n_grp, dtype=jnp.int32)
    q_ids = jnp.arange(per_row, dtype=jnp.int32)

    by_d = {}
    prev = None
    for k in range(len(sizes)):
        per_chunk = sizes[k]
        lo = starts[k]
        pos_ids = jnp.arange(per_chunk, dtype=jnp.int32)
        rows_at = [[(b + lo + dl) % ACT for dl in range(per_chunk)] for b in range(n_mem)]
        left = blocks[:, jnp.array(rows_at, dtype=jnp.int32)]
        piece = jnp.einsum("nbdk,nbl->bdkl", left, blocks, preferred_element_type=jnp.float32)
        if prev is not None:
            piece, prev = lax.optimization_barrier((piece, prev))
        else:
            row0 = jnp.einsum("nk,nbl->bkl", blocks[:, 0], blocks, preferred_element_type=jnp.float32)
            piece = jnp.concatenate([piece, row0[:, None]], axis=1)
            piece = jnp.concatenate([piece, id_rows], axis=2)
        got_piece = lax.all_to_all(piece, "mem", split_axis=0, concat_axis=0, tiled=True)
        if prev is None:
            everyone = got_piece[:, 0, BLK, :ACT].astype(jnp.int32)
            got_piece = got_piece[:, :, :BLK]
            row_grp = everyone // 8
            col_grp = jnp.take(everyone, member, axis=1) // 8
            zero_on = everyone[:, 0] == 0
            row0_got = got_piece[:, per_chunk]
            got_piece = got_piece[:, :per_chunk]
        prev = got_piece
        flat = got_piece.reshape(n_mem * per_chunk, BLK * BLK)
        apos = (member + lo + pos_ids) % ACT
        rg = jnp.take(row_grp, apos, axis=1)
        sel = (
            (pos_ids[None, :, None, None, None] == pos_ids[None, None, None, None, :])
            & (rg[None, None, None, :, :] == grp_ids[:, None, None, None, None])
            & (col_grp[None, None, None, :, None] == q_ids[None, None, :, None, None])
        )
        if lo >= tail:
            sel = jnp.stack([sel[g][:, [q for q in range(per_row) if q != g]] for g in range(n_grp)])
        kept = sel.shape[2]
        sel = sel.reshape(n_grp, per_chunk * kept, n_mem * per_chunk)
        if k == 0:
            col_sel = (
                (col_grp[None, :] == grp_ids[:, None]) & zero_on[None, :]
            ).astype(jnp.float32)
            col_part = jnp.dot(
                col_sel, row0_got.reshape(n_mem, BLK * BLK), precision=HI,
                preferred_element_type=jnp.float32,
            ).reshape(n_grp, 1, BLK * BLK)
        send = jnp.dot(
            sel.reshape(n_grp * per_chunk * kept, n_mem * per_chunk).astype(jnp.float32),
            flat,
            precision=HI,
            preferred_element_type=jnp.float32,
        ).reshape(n_grp, per_chunk * kept, BLK * BLK)
        if k == 0:
            send = jnp.concatenate([send, col_part], axis=1)
        width = send.shape[1]
        got = lax.psum_scatter(
            send.reshape(n_grp * width, BLK, BLK), "grp", scatter_dimension=0, tiled=True
        )
        if k == 0:
            col_tile = jnp.transpose(got[per_chunk * kept]) / divisor
            got = got[: per_chunk * kept]
        got = got.reshape(per_chunk, kept, BLK, BLK)
        for dl in range(per_chunk):
            by_d[lo + dl] = got[dl]

    for d in range(tail, ACT):
        shift = ACT - d
        src_tile = jnp.transpose(jnp.take(by_d[shift], group, axis=0))
        moved = lax.ppermute(
            src_tile, "mem", perm=[(j, (j + shift) % n_mem) for j in range(n_mem)]
        )
        others = by_d[d]
        q_pos = jnp.clip(q_ids - (q_ids > group).astype(jnp.int32), 0, per_row - 2)
        spread = jnp.take(others, q_pos, axis=0)
        by_d[d] = jnp.where((q_ids == group)[:, None, None], moved[None], spread)
    owned_d = jnp.stack([by_d[d] for d in range(ACT)])
    owned = jnp.roll(owned_d, member, axis=0).reshape(ACT * per_row, BLK, BLK)

    col_tile, prev = lax.optimization_barrier((col_tile, prev))
    spread = jnp.broadcast_to(col_tile[None], (n_grp, BLK, BLK))
    col_cols = lax.all_to_all(spread, "grp", split_axis=0, concat_axis=0, tiled=True)
    pair = jnp.broadcast_to(jnp.stack([col_tile, col_cols[0]])[None], (n_mem, 2, BLK, BLK))
    pairs = lax.all_to_all(pair, "mem", split_axis=0, concat_axis=0, tiled=True)
    col_rows = pairs[:, 0]
    a00 = pairs[0, 1] + eye * ridge_blocks[0][None, :]
    chol = jnp.linalg.cholesky(a00)
    chol_inv = lax.linalg.triangular_solve(chol, eye, left_side=True, lower=True)

    t = jnp.arange(ACT * per_row, dtype=jnp.int32)
    tile_rows = group * 8 + t // per_row
    tile_cols = (t % per_row) * 8 + member
    same = (tile_rows == tile_cols).astype(jnp.float32)
    diag = eye[None] * jnp.take(ridge_blocks, tile_rows, axis=0)[:, None, :] * same[:, None, None]
    tiles = owned / divisor + diag

    p_rows = jnp.einsum("ipr,qr->ipq", col_rows, chol_inv, precision=HI)
    p_cols = jnp.einsum("ipr,qr->ipq", col_cols, chol_inv, precision=HI)
    row_ids = group * 8 + jnp.arange(8, dtype=jnp.int32)
    col_ids = jnp.arange(per_row, dtype=jnp.int32) * 8 + member
    p_rows = jnp.where((row_ids == 0)[:, None, None], chol[None], p_rows)
    p_cols = jnp.where((col_ids == 0)[:, None, None], chol[None], p_cols)

    update = jnp.einsum("apr,qsr->aqps", p_rows, p_cols, precision=HI)
    update = update.reshape(ACT * per_row, BLK, BLK)
    left_tiles = jnp.repeat(p_rows, per_row, axis=0)
    right_tiles = jnp.tile(p_cols, (ACT, 1, 1))
    trailing = ((tile_rows > 0) & (tile_cols > 0))[:, None, None]
    on_column = (tile_cols == 0)[:, None, None]
    on_row = ((tile_rows == 0) & (tile_cols > 0))[:, None, None]
    tiles = jnp.where(trailing, tiles - update, tiles)
    tiles = jnp.where(on_column, left_tiles, tiles)
    tiles = jnp.where(on_row, jnp.transpose(right_tiles, (0, 2, 1)), tiles)
    return tiles[None]


def solution(mesh):
    n_mem = mesh.shape["mem"]
    n_grp = mesh.shape["grp"]
    fast = n_mem == 8 and n_grp * 8 == NB
    body = on_device_fast if fast else on_device_general
    in_specs = (P(("grp", "mem"), None), P(("grp", "mem"), None), P())
    out_specs = P("mem", "grp", None, None)
    return jax.shard_map(
        body, mesh=mesh, in_specs=in_specs, out_specs=out_specs, check_vma=False
    )
```

```python
import jax
import jax.numpy as jnp
from jax import lax
from jax.sharding import PartitionSpec as P

NB = 32
BLK = 128
ACT = 8
HI = lax.Precision.HIGHEST


def panel_solve(column):
    count = column.shape[0]
    chol = jnp.linalg.cholesky(column[0])
    stacked = jnp.transpose(column, (2, 0, 1)).reshape(BLK, count * BLK)
    solved = lax.linalg.triangular_solve(chol, stacked, left_side=True, lower=True)
    lower_col = jnp.transpose(solved.reshape(BLK, count, BLK), (1, 2, 0))
    return lower_col.at[0].set(chol)


def apply_step(tiles, lower_col, step, tile_rows, tile_cols):
    left_tiles = jnp.take(lower_col, jnp.maximum(tile_rows - step, 0), axis=0)
    right_tiles = jnp.take(lower_col, jnp.maximum(tile_cols - step, 0), axis=0)
    update = jnp.einsum("tpr,tqr->tpq", left_tiles, right_tiles, precision=HI)
    trailing = ((tile_rows > step) & (tile_cols > step))[:, None, None]
    on_column = ((tile_cols == step) & (tile_rows >= step))[:, None, None]
    on_row = ((tile_rows == step) & (tile_cols > step))[:, None, None]
    tiles = jnp.where(trailing, tiles - update, tiles)
    tiles = jnp.where(on_column, left_tiles, tiles)
    tiles = jnp.where(on_row, jnp.transpose(right_tiles, (0, 2, 1)), tiles)
    return tiles


def column_picker(step, tile_rows, tile_cols):
    wanted = step + jnp.arange(NB - step, dtype=jnp.int32)
    inside = (tile_cols == step) & (tile_rows >= step)
    return ((tile_rows[None, :] == wanted[:, None]) & inside[None, :]).astype(jnp.float32)


def on_device_general(design, active_blocks, ridge):
    n_mem = lax.axis_size("mem")
    n_grp = lax.axis_size("grp")
    member = lax.axis_index("mem")
    group = lax.axis_index("grp")
    classes = n_mem // 8
    per_pos = ACT // classes
    per_row = NB // ACT
    slot_count = NB // classes * per_row
    owned_count = slot_count // n_grp
    row_count = design.shape[0]
    residue = member // 8
    position = member % 8
    everyone = lax.all_gather(active_blocks, "mem", axis=0, tiled=True)
    blocks = design.reshape(row_count, ACT, BLK)
    left = blocks.reshape(row_count, per_pos, classes, BLK)
    outgoing = jnp.einsum("ncqk,nbl->qbckl", left, blocks, preferred_element_type=jnp.float32)
    outgoing = outgoing.reshape(n_mem, per_pos, BLK, BLK)
    received = lax.all_to_all(outgoing, "mem", split_axis=0, concat_axis=0, tiled=True)
    row_ids = jnp.take(everyone.reshape(n_mem, per_pos, classes), residue, axis=2)
    col_ids = jnp.take(everyone, position, axis=1)
    targets = row_ids // classes * per_row + (col_ids // 8)[:, None]
    onehot = (
        targets.reshape(-1)[None, :] == jnp.arange(slot_count, dtype=jnp.int32)[:, None]
    ).astype(jnp.float32)
    sums = jnp.dot(
        onehot,
        received.reshape(n_mem * per_pos, BLK * BLK),
        precision=HI,
        preferred_element_type=jnp.float32,
    )
    sums = sums.reshape(slot_count, BLK, BLK)
    owned = lax.psum_scatter(sums, "grp", scatter_dimension=0, tiled=True)
    slots = group * owned_count + jnp.arange(owned_count, dtype=jnp.int32)
    tile_rows = slots // per_row * classes + residue
    tile_cols = slots % per_row * 8 + position
    ridge_blocks = jnp.take(ridge.reshape(NB, BLK), tile_rows, axis=0)
    same = (tile_rows == tile_cols).astype(jnp.float32)
    extra = jnp.eye(BLK, dtype=jnp.float32)[None] * ridge_blocks[:, None, :] * same[:, None, None]
    divisor = jnp.float32(row_count * n_grp * n_mem // 16)
    tiles = owned / divisor + extra
    picker = column_picker(0, tile_rows, tile_cols)
    partial_value = jnp.einsum("it,tpq->ipq", picker, tiles, precision=HI)
    column = lax.psum(partial_value, ("grp", "mem"))
    lower_col = panel_solve(column)
    tiles = apply_step(tiles, lower_col, 0, tile_rows, tile_cols)
    return tiles[None]


def on_device_fast(design, active_blocks, ridge):
    n_mem = lax.axis_size("mem")
    n_grp = lax.axis_size("grp")
    member = lax.axis_index("mem")
    group = lax.axis_index("grp")
    per_row = NB // ACT
    sizes = (1, 2, 2, 3)
    starts = (0, 1, 3, 5)
    tail = starts[-1]
    row_count = design.shape[0]
    divisor = jnp.float32(row_count * n_grp * n_mem // 16)
    eye = jnp.eye(BLK, dtype=jnp.float32)
    ridge_blocks = ridge.reshape(NB, BLK)

    blocks = design.reshape(row_count, ACT, BLK)
    id_rows = jnp.zeros((8, BLK), jnp.float32).at[0, :ACT].set(active_blocks[0].astype(jnp.float32))
    id_rows = jnp.broadcast_to(id_rows[None, None], (n_mem, 1, 8, BLK))
    grp_ids = jnp.arange(n_grp, dtype=jnp.int32)
    q_ids = jnp.arange(per_row, dtype=jnp.int32)

    by_d = {}
    prev = None
    for k in range(len(sizes)):
        per_chunk = sizes[k]
        lo = starts[k]
        pos_ids = jnp.arange(per_chunk, dtype=jnp.int32)
        rows_at = [[(b + lo + dl) % ACT for dl in range(per_chunk)] for b in range(n_mem)]
        left = blocks[:, jnp.array(rows_at, dtype=jnp.int32)]
        piece = jnp.einsum("nbdk,nbl->bdkl", left, blocks, preferred_element_type=jnp.float32)
        if k == 1:
            row0 = jnp.einsum("nk,nbl->bkl", blocks[:, 0], blocks, preferred_element_type=jnp.float32)
            piece = jnp.concatenate([piece, row0[:, None]], axis=1)
        if prev is not None:
            piece, prev = lax.optimization_barrier((piece, prev))
        else:
            piece = jnp.concatenate([piece, id_rows], axis=2)
        got_piece = lax.all_to_all(piece, "mem", split_axis=0, concat_axis=0, tiled=True)
        if prev is None:
            everyone = got_piece[:, 0, BLK, :ACT].astype(jnp.int32)
            got_piece = got_piece[:, :, :BLK]
            row_grp = everyone // 8
            col_grp = jnp.take(everyone, member, axis=1) // 8
            zero_on = everyone[:, 0] == 0
        if k == 1:
            row0_got = got_piece[:, per_chunk]
            got_piece = got_piece[:, :per_chunk]
        prev = got_piece
        flat = got_piece.reshape(n_mem * per_chunk, BLK * BLK)
        apos = (member + lo + pos_ids) % ACT
        rg = jnp.take(row_grp, apos, axis=1)
        sel = (
            (pos_ids[None, :, None, None, None] == pos_ids[None, None, None, None, :])
            & (rg[None, None, None, :, :] == grp_ids[:, None, None, None, None])
            & (col_grp[None, None, None, :, None] == q_ids[None, None, :, None, None])
        )
        if lo >= tail:
            sel = jnp.stack([sel[g][:, [q for q in range(per_row) if q != g]] for g in range(n_grp)])
        kept = sel.shape[2]
        sel = sel.reshape(n_grp, per_chunk * kept, n_mem * per_chunk)
        if k == 1:
            col_sel = (
                (col_grp[None, :] == grp_ids[:, None]) & zero_on[None, :]
            ).astype(jnp.float32)
            col_part = jnp.dot(
                col_sel, row0_got.reshape(n_mem, BLK * BLK), precision=HI,
                preferred_element_type=jnp.float32,
            ).reshape(n_grp, 1, BLK * BLK)
        send = jnp.dot(
            sel.reshape(n_grp * per_chunk * kept, n_mem * per_chunk).astype(jnp.float32),
            flat,
            precision=HI,
            preferred_element_type=jnp.float32,
        ).reshape(n_grp, per_chunk * kept, BLK * BLK)
        if k == 1:
            send = jnp.concatenate([send, col_part], axis=1)
        width = send.shape[1]
        got = lax.psum_scatter(
            send.reshape(n_grp * width, BLK, BLK), "grp", scatter_dimension=0, tiled=True
        )
        if k == 1:
            col_tile = jnp.transpose(got[per_chunk * kept]) / divisor
            got = got[: per_chunk * kept]
        got = got.reshape(per_chunk, kept, BLK, BLK)
        for dl in range(per_chunk):
            by_d[lo + dl] = got[dl]

    for d in range(tail, ACT):
        shift = ACT - d
        src_tile = jnp.transpose(jnp.take(by_d[shift], group, axis=0))
        moved = lax.ppermute(
            src_tile, "mem", perm=[(j, (j + shift) % n_mem) for j in range(n_mem)]
        )
        others = by_d[d]
        slots = []
        for q in range(per_row):
            below = others[min(q, per_row - 2)]
            above = others[max(q - 1, 0)]
            slots.append(jnp.where(q == group, moved, jnp.where(q < group, below, above)))
        by_d[d] = jnp.stack(slots)
    owned = jnp.stack([by_d[d] for d in range(ACT)]).reshape(ACT * per_row, BLK, BLK)

    col_tile, prev = lax.optimization_barrier((col_tile, prev))
    spread = jnp.broadcast_to(col_tile[None], (n_grp, BLK, BLK))
    col_cols = lax.all_to_all(spread, "grp", split_axis=0, concat_axis=0, tiled=True)
    pair = jnp.broadcast_to(jnp.stack([col_tile, col_cols[0]])[None], (n_mem, 2, BLK, BLK))
    pairs = lax.all_to_all(pair, "mem", split_axis=0, concat_axis=0, tiled=True)
    col_rows = pairs[:, 0]
    a00 = pairs[0, 1] + eye * ridge_blocks[0][None, :]
    chol = jnp.linalg.cholesky(a00)
    chol_inv = lax.linalg.triangular_solve(chol, eye, left_side=True, lower=True)

    a_of_d = (member + jnp.arange(ACT, dtype=jnp.int32)) % ACT
    t = jnp.arange(ACT * per_row, dtype=jnp.int32)
    tile_rows = group * 8 + jnp.take(a_of_d, t // per_row)
    tile_cols = (t % per_row) * 8 + member
    same = (tile_rows == tile_cols).astype(jnp.float32)
    diag = eye[None] * jnp.take(ridge_blocks, tile_rows, axis=0)[:, None, :] * same[:, None, None]
    tiles = owned / divisor + diag

    p_rows = jnp.einsum("ipr,qr->ipq", col_rows, chol_inv, precision=HI)
    p_cols = jnp.einsum("ipr,qr->ipq", col_cols, chol_inv, precision=HI)
    p_rows = jnp.take(p_rows, a_of_d, axis=0)
    row_ids = group * 8 + a_of_d
    col_ids = jnp.arange(per_row, dtype=jnp.int32) * 8 + member
    p_rows = jnp.where((row_ids == 0)[:, None, None], chol[None], p_rows)
    p_cols = jnp.where((col_ids == 0)[:, None, None], chol[None], p_cols)

    update = jnp.einsum("apr,qsr->aqps", p_rows, p_cols, precision=HI)
    update = update.reshape(ACT * per_row, BLK, BLK)
    left_tiles = jnp.repeat(p_rows, per_row, axis=0)
    right_tiles = jnp.tile(p_cols, (ACT, 1, 1))
    trailing = ((tile_rows > 0) & (tile_cols > 0))[:, None, None]
    on_column = (tile_cols == 0)[:, None, None]
    on_row = ((tile_rows == 0) & (tile_cols > 0))[:, None, None]
    tiles = jnp.where(trailing, tiles - update, tiles)
    tiles = jnp.where(on_column, left_tiles, tiles)
    tiles = jnp.where(on_row, jnp.transpose(right_tiles, (0, 2, 1)), tiles)
    tiles = jnp.roll(tiles.reshape(ACT, per_row, BLK, BLK), member, axis=0)
    return tiles.reshape(1, ACT * per_row, BLK, BLK)


def solution(mesh):
    n_mem = mesh.shape["mem"]
    n_grp = mesh.shape["grp"]
    fast = n_mem == 8 and n_grp * 8 == NB
    body = on_device_fast if fast else on_device_general
    in_specs = (P(("grp", "mem"), None), P(("grp", "mem"), None), P())
    out_specs = P("mem", "grp", None, None)
    return jax.shard_map(
        body, mesh=mesh, in_specs=in_specs, out_specs=out_specs, check_vma=False
    )
```

```python
import jax
import jax.numpy as jnp
from jax import lax
from jax.sharding import PartitionSpec as P

NB = 32
BLK = 128
ACT = 8
HI = lax.Precision.HIGHEST


def panel_solve(column):
    count = column.shape[0]
    chol = jnp.linalg.cholesky(column[0])
    stacked = jnp.transpose(column, (2, 0, 1)).reshape(BLK, count * BLK)
    solved = lax.linalg.triangular_solve(chol, stacked, left_side=True, lower=True)
    lower_col = jnp.transpose(solved.reshape(BLK, count, BLK), (1, 2, 0))
    return lower_col.at[0].set(chol)


def apply_step(tiles, lower_col, step, tile_rows, tile_cols):
    left_tiles = jnp.take(lower_col, jnp.maximum(tile_rows - step, 0), axis=0)
    right_tiles = jnp.take(lower_col, jnp.maximum(tile_cols - step, 0), axis=0)
    update = jnp.einsum("tpr,tqr->tpq", left_tiles, right_tiles, precision=HI)
    trailing = ((tile_rows > step) & (tile_cols > step))[:, None, None]
    on_column = ((tile_cols == step) & (tile_rows >= step))[:, None, None]
    on_row = ((tile_rows == step) & (tile_cols > step))[:, None, None]
    tiles = jnp.where(trailing, tiles - update, tiles)
    tiles = jnp.where(on_column, left_tiles, tiles)
    tiles = jnp.where(on_row, jnp.transpose(right_tiles, (0, 2, 1)), tiles)
    return tiles


def column_picker(step, tile_rows, tile_cols):
    wanted = step + jnp.arange(NB - step, dtype=jnp.int32)
    inside = (tile_cols == step) & (tile_rows >= step)
    return ((tile_rows[None, :] == wanted[:, None]) & inside[None, :]).astype(jnp.float32)


def on_device_general(design, active_blocks, ridge):
    n_mem = lax.axis_size("mem")
    n_grp = lax.axis_size("grp")
    member = lax.axis_index("mem")
    group = lax.axis_index("grp")
    classes = n_mem // 8
    per_pos = ACT // classes
    per_row = NB // ACT
    slot_count = NB // classes * per_row
    owned_count = slot_count // n_grp
    row_count = design.shape[0]
    residue = member // 8
    position = member % 8
    everyone = lax.all_gather(active_blocks, "mem", axis=0, tiled=True)
    blocks = design.reshape(row_count, ACT, BLK)
    left = blocks.reshape(row_count, per_pos, classes, BLK)
    outgoing = jnp.einsum("ncqk,nbl->qbckl", left, blocks, preferred_element_type=jnp.float32)
    outgoing = outgoing.reshape(n_mem, per_pos, BLK, BLK)
    received = lax.all_to_all(outgoing, "mem", split_axis=0, concat_axis=0, tiled=True)
    row_ids = jnp.take(everyone.reshape(n_mem, per_pos, classes), residue, axis=2)
    col_ids = jnp.take(everyone, position, axis=1)
    targets = row_ids // classes * per_row + (col_ids // 8)[:, None]
    onehot = (
        targets.reshape(-1)[None, :] == jnp.arange(slot_count, dtype=jnp.int32)[:, None]
    ).astype(jnp.float32)
    sums = jnp.dot(
        onehot,
        received.reshape(n_mem * per_pos, BLK * BLK),
        precision=HI,
        preferred_element_type=jnp.float32,
    )
    sums = sums.reshape(slot_count, BLK, BLK)
    owned = lax.psum_scatter(sums, "grp", scatter_dimension=0, tiled=True)
    slots = group * owned_count + jnp.arange(owned_count, dtype=jnp.int32)
    tile_rows = slots // per_row * classes + residue
    tile_cols = slots % per_row * 8 + position
    ridge_blocks = jnp.take(ridge.reshape(NB, BLK), tile_rows, axis=0)
    same = (tile_rows == tile_cols).astype(jnp.float32)
    extra = jnp.eye(BLK, dtype=jnp.float32)[None] * ridge_blocks[:, None, :] * same[:, None, None]
    divisor = jnp.float32(row_count * n_grp * n_mem // 16)
    tiles = owned / divisor + extra
    picker = column_picker(0, tile_rows, tile_cols)
    partial_value = jnp.einsum("it,tpq->ipq", picker, tiles, precision=HI)
    column = lax.psum(partial_value, ("grp", "mem"))
    lower_col = panel_solve(column)
    tiles = apply_step(tiles, lower_col, 0, tile_rows, tile_cols)
    return tiles[None]


def on_device_fast(design, active_blocks, ridge):
    n_mem = lax.axis_size("mem")
    n_grp = lax.axis_size("grp")
    member = lax.axis_index("mem")
    group = lax.axis_index("grp")
    per_row = NB // ACT
    sizes = (1, 3, 4)
    starts = (0, 1, 4)
    row_count = design.shape[0]
    divisor = jnp.float32(row_count * n_grp * n_mem // 16)
    eye = jnp.eye(BLK, dtype=jnp.float32)
    ridge_blocks = ridge.reshape(NB, BLK)

    blocks = design.reshape(row_count, ACT, BLK)
    id_rows = jnp.zeros((8, BLK), jnp.float32).at[0, :ACT].set(active_blocks[0].astype(jnp.float32))
    id_rows = jnp.broadcast_to(id_rows[None, None], (n_mem, 1, 8, BLK))
    grp_ids = jnp.arange(n_grp, dtype=jnp.int32)
    q_ids = jnp.arange(per_row, dtype=jnp.int32)

    owned_parts = []
    prev = None
    for k in range(len(sizes)):
        per_chunk = sizes[k]
        lo = starts[k]
        pos_ids = jnp.arange(per_chunk, dtype=jnp.int32)
        piece = jnp.einsum(
            "nak,nbl->bakl", blocks[:, lo:lo + per_chunk], blocks, preferred_element_type=jnp.float32
        )
        if prev is not None:
            piece, prev = lax.optimization_barrier((piece, prev))
        else:
            piece = jnp.concatenate([piece, id_rows], axis=2)
        got_piece = lax.all_to_all(piece, "mem", split_axis=0, concat_axis=0, tiled=True)
        if prev is None:
            everyone = got_piece[:, 0, BLK, :ACT].astype(jnp.int32)
            got_piece = got_piece[:, :, :BLK]
            row_grp = everyone // 8
            col_grp = jnp.take(everyone, member, axis=1) // 8
            zero_on = everyone[:, 0] == 0
        got_piece = got_piece.reshape(n_mem, per_chunk, BLK, BLK)
        prev = got_piece
        rg = row_grp[:, lo:lo + per_chunk]
        sel = (
            (pos_ids[None, :, None, None, None] == pos_ids[None, None, None, None, :])
            & (rg[None, None, None, :, :] == grp_ids[:, None, None, None, None])
            & (col_grp[None, None, None, :, None] == q_ids[None, None, :, None, None])
        )
        sel = sel.reshape(n_grp, per_chunk * per_row, n_mem * per_chunk)
        if k == 0:
            first = pos_ids == 0
            col_sel = (
                (col_grp[None, :, None] == grp_ids[:, None, None])
                & zero_on[None, :, None]
                & first[None, None, :]
            ).reshape(n_grp, 1, n_mem * per_chunk)
            sel = jnp.concatenate([sel, col_sel], axis=1)
        width = sel.shape[1]
        send = jnp.dot(
            sel.reshape(n_grp * width, n_mem * per_chunk).astype(jnp.float32),
            got_piece.reshape(n_mem * per_chunk, BLK * BLK),
            precision=HI,
            preferred_element_type=jnp.float32,
        ).reshape(n_grp * width, BLK, BLK)
        got = lax.psum_scatter(send, "grp", scatter_dimension=0, tiled=True)
        owned_parts.append(got[: per_chunk * per_row])
        if k == 0:
            col_tile = jnp.transpose(got[per_chunk * per_row]) / divisor
    owned = jnp.concatenate(owned_parts, axis=0)

    col_tile, prev = lax.optimization_barrier((col_tile, prev))
    spread = jnp.broadcast_to(col_tile[None], (n_grp, BLK, BLK))
    col_cols = lax.all_to_all(spread, "grp", split_axis=0, concat_axis=0, tiled=True)
    pair = jnp.broadcast_to(jnp.stack([col_tile, col_cols[0]])[None], (n_mem, 2, BLK, BLK))
    pairs = lax.all_to_all(pair, "mem", split_axis=0, concat_axis=0, tiled=True)
    col_rows = pairs[:, 0]
    a00 = pairs[0, 1] + eye * ridge_blocks[0][None, :]
    chol = jnp.linalg.cholesky(a00)
    chol_inv = lax.linalg.triangular_solve(chol, eye, left_side=True, lower=True)

    t = jnp.arange(ACT * per_row, dtype=jnp.int32)
    tile_rows = group * 8 + t // per_row
    tile_cols = (t % per_row) * 8 + member
    same = (tile_rows == tile_cols).astype(jnp.float32)
    diag = eye[None] * jnp.take(ridge_blocks, tile_rows, axis=0)[:, None, :] * same[:, None, None]
    tiles = owned / divisor + diag

    p_rows = jnp.einsum("ipr,qr->ipq", col_rows, chol_inv, precision=HI)
    p_cols = jnp.einsum("ipr,qr->ipq", col_cols, chol_inv, precision=HI)
    row_ids = group * 8 + jnp.arange(8, dtype=jnp.int32)
    col_ids = jnp.arange(per_row, dtype=jnp.int32) * 8 + member
    p_rows = jnp.where((row_ids == 0)[:, None, None], chol[None], p_rows)
    p_cols = jnp.where((col_ids == 0)[:, None, None], chol[None], p_cols)

    update = jnp.einsum("apr,qsr->aqps", p_rows, p_cols, precision=HI)
    update = update.reshape(ACT * per_row, BLK, BLK)
    left_tiles = jnp.repeat(p_rows, per_row, axis=0)
    right_tiles = jnp.tile(p_cols, (ACT, 1, 1))
    trailing = ((tile_rows > 0) & (tile_cols > 0))[:, None, None]
    on_column = (tile_cols == 0)[:, None, None]
    on_row = ((tile_rows == 0) & (tile_cols > 0))[:, None, None]
    tiles = jnp.where(trailing, tiles - update, tiles)
    tiles = jnp.where(on_column, left_tiles, tiles)
    tiles = jnp.where(on_row, jnp.transpose(right_tiles, (0, 2, 1)), tiles)
    return tiles[None]


def solution(mesh):
    n_mem = mesh.shape["mem"]
    n_grp = mesh.shape["grp"]
    fast = n_mem == 8 and n_grp * 8 == NB
    body = on_device_fast if fast else on_device_general
    in_specs = (P(("grp", "mem"), None), P(("grp", "mem"), None), P())
    out_specs = P("mem", "grp", None, None)
    return jax.shard_map(
        body, mesh=mesh, in_specs=in_specs, out_specs=out_specs, check_vma=False
    )
```

```python
import jax
import jax.numpy as jnp
from jax import lax
from jax.sharding import PartitionSpec as P

NB = 32
BLK = 128
ACT = 8
HI = lax.Precision.HIGHEST


def panel_solve(column):
    count = column.shape[0]
    chol = jnp.linalg.cholesky(column[0])
    stacked = jnp.transpose(column, (2, 0, 1)).reshape(BLK, count * BLK)
    solved = lax.linalg.triangular_solve(chol, stacked, left_side=True, lower=True)
    lower_col = jnp.transpose(solved.reshape(BLK, count, BLK), (1, 2, 0))
    return lower_col.at[0].set(chol)


def apply_step(tiles, lower_col, step, tile_rows, tile_cols):
    left_tiles = jnp.take(lower_col, jnp.maximum(tile_rows - step, 0), axis=0)
    right_tiles = jnp.take(lower_col, jnp.maximum(tile_cols - step, 0), axis=0)
    update = jnp.einsum("tpr,tqr->tpq", left_tiles, right_tiles, precision=HI)
    trailing = ((tile_rows > step) & (tile_cols > step))[:, None, None]
    on_column = ((tile_cols == step) & (tile_rows >= step))[:, None, None]
    on_row = ((tile_rows == step) & (tile_cols > step))[:, None, None]
    tiles = jnp.where(trailing, tiles - update, tiles)
    tiles = jnp.where(on_column, left_tiles, tiles)
    tiles = jnp.where(on_row, jnp.transpose(right_tiles, (0, 2, 1)), tiles)
    return tiles


def column_picker(step, tile_rows, tile_cols):
    wanted = step + jnp.arange(NB - step, dtype=jnp.int32)
    inside = (tile_cols == step) & (tile_rows >= step)
    return ((tile_rows[None, :] == wanted[:, None]) & inside[None, :]).astype(jnp.float32)


def on_device_general(design, active_blocks, ridge):
    n_mem = lax.axis_size("mem")
    n_grp = lax.axis_size("grp")
    member = lax.axis_index("mem")
    group = lax.axis_index("grp")
    classes = n_mem // 8
    per_pos = ACT // classes
    per_row = NB // ACT
    slot_count = NB // classes * per_row
    owned_count = slot_count // n_grp
    row_count = design.shape[0]
    residue = member // 8
    position = member % 8
    everyone = lax.all_gather(active_blocks, "mem", axis=0, tiled=True)
    blocks = design.reshape(row_count, ACT, BLK)
    left = blocks.reshape(row_count, per_pos, classes, BLK)
    outgoing = jnp.einsum("ncqk,nbl->qbckl", left, blocks, preferred_element_type=jnp.float32)
    outgoing = outgoing.reshape(n_mem, per_pos, BLK, BLK)
    received = lax.all_to_all(outgoing, "mem", split_axis=0, concat_axis=0, tiled=True)
    row_ids = jnp.take(everyone.reshape(n_mem, per_pos, classes), residue, axis=2)
    col_ids = jnp.take(everyone, position, axis=1)
    targets = row_ids // classes * per_row + (col_ids // 8)[:, None]
    onehot = (
        targets.reshape(-1)[None, :] == jnp.arange(slot_count, dtype=jnp.int32)[:, None]
    ).astype(jnp.float32)
    sums = jnp.dot(
        onehot,
        received.reshape(n_mem * per_pos, BLK * BLK),
        precision=HI,
        preferred_element_type=jnp.float32,
    )
    sums = sums.reshape(slot_count, BLK, BLK)
    owned = lax.psum_scatter(sums, "grp", scatter_dimension=0, tiled=True)
    slots = group * owned_count + jnp.arange(owned_count, dtype=jnp.int32)
    tile_rows = slots // per_row * classes + residue
    tile_cols = slots % per_row * 8 + position
    ridge_blocks = jnp.take(ridge.reshape(NB, BLK), tile_rows, axis=0)
    same = (tile_rows == tile_cols).astype(jnp.float32)
    extra = jnp.eye(BLK, dtype=jnp.float32)[None] * ridge_blocks[:, None, :] * same[:, None, None]
    divisor = jnp.float32(row_count * n_grp * n_mem // 16)
    tiles = owned / divisor + extra
    picker = column_picker(0, tile_rows, tile_cols)
    partial_value = jnp.einsum("it,tpq->ipq", picker, tiles, precision=HI)
    column = lax.psum(partial_value, ("grp", "mem"))
    lower_col = panel_solve(column)
    tiles = apply_step(tiles, lower_col, 0, tile_rows, tile_cols)
    return tiles[None]


def on_device_fast(design, active_blocks, ridge):
    n_mem = lax.axis_size("mem")
    n_grp = lax.axis_size("grp")
    member = lax.axis_index("mem")
    group = lax.axis_index("grp")
    per_row = NB // ACT
    sizes = (2, 6)
    starts = (0, 2)
    row_count = design.shape[0]
    divisor = jnp.float32(row_count * n_grp * n_mem // 16)
    eye = jnp.eye(BLK, dtype=jnp.float32)
    ridge_blocks = ridge.reshape(NB, BLK)

    blocks = design.reshape(row_count, ACT, BLK)
    id_rows = jnp.zeros((8, BLK), jnp.float32).at[0, :ACT].set(active_blocks[0].astype(jnp.float32))
    id_rows = jnp.broadcast_to(id_rows[None, None], (n_mem, 1, 8, BLK))
    grp_ids = jnp.arange(n_grp, dtype=jnp.int32)
    q_ids = jnp.arange(per_row, dtype=jnp.int32)

    owned_parts = []
    prev = None
    for k in range(len(sizes)):
        per_chunk = sizes[k]
        lo = starts[k]
        pos_ids = jnp.arange(per_chunk, dtype=jnp.int32)
        piece = jnp.einsum(
            "nak,nbl->bakl", blocks[:, lo:lo + per_chunk], blocks, preferred_element_type=jnp.float32
        )
        if prev is not None:
            piece, prev = lax.optimization_barrier((piece, prev))
        else:
            ids_here = jnp.broadcast_to(id_rows, (n_mem, per_chunk, 8, BLK))
            piece = jnp.concatenate([piece, ids_here], axis=2)
        got_piece = lax.all_to_all(piece, "mem", split_axis=0, concat_axis=0, tiled=True)
        if prev is None:
            everyone = got_piece[:, 0, BLK, :ACT].astype(jnp.int32)
            got_piece = got_piece[:, :, :BLK]
            row_grp = everyone // 8
            col_grp = jnp.take(everyone, member, axis=1) // 8
            zero_on = everyone[:, 0] == 0
        got_piece = got_piece.reshape(n_mem, per_chunk, BLK, BLK)
        prev = got_piece
        rg = row_grp[:, lo:lo + per_chunk]
        sel = (
            (pos_ids[None, :, None, None, None] == pos_ids[None, None, None, None, :])
            & (rg[None, None, None, :, :] == grp_ids[:, None, None, None, None])
            & (col_grp[None, None, None, :, None] == q_ids[None, None, :, None, None])
        )
        sel = sel.reshape(n_grp, per_chunk * per_row, n_mem * per_chunk)
        if k == 0:
            first = pos_ids == 0
            col_sel = (
                (col_grp[None, :, None] == grp_ids[:, None, None])
                & zero_on[None, :, None]
                & first[None, None, :]
            ).reshape(n_grp, 1, n_mem * per_chunk)
            sel = jnp.concatenate([sel, col_sel], axis=1)
        width = sel.shape[1]
        send = jnp.dot(
            sel.reshape(n_grp * width, n_mem * per_chunk).astype(jnp.float32),
            got_piece.reshape(n_mem * per_chunk, BLK * BLK),
            precision=HI,
            preferred_element_type=jnp.float32,
        ).reshape(n_grp * width, BLK, BLK)
        got = lax.psum_scatter(send, "grp", scatter_dimension=0, tiled=True)
        owned_parts.append(got[: per_chunk * per_row])
        if k == 0:
            col_tile = jnp.transpose(got[per_chunk * per_row]) / divisor
    owned = jnp.concatenate(owned_parts, axis=0)

    col_tile, prev = lax.optimization_barrier((col_tile, prev))
    spread = jnp.broadcast_to(col_tile[None], (n_grp, BLK, BLK))
    col_cols = lax.all_to_all(spread, "grp", split_axis=0, concat_axis=0, tiled=True)
    pair = jnp.broadcast_to(jnp.stack([col_tile, col_cols[0]])[None], (n_mem, 2, BLK, BLK))
    pairs = lax.all_to_all(pair, "mem", split_axis=0, concat_axis=0, tiled=True)
    col_rows = pairs[:, 0]
    a00 = pairs[0, 1] + eye * ridge_blocks[0][None, :]
    chol = jnp.linalg.cholesky(a00)
    chol_inv = lax.linalg.triangular_solve(chol, eye, left_side=True, lower=True)

    t = jnp.arange(ACT * per_row, dtype=jnp.int32)
    tile_rows = group * 8 + t // per_row
    tile_cols = (t % per_row) * 8 + member
    same = (tile_rows == tile_cols).astype(jnp.float32)
    diag = eye[None] * jnp.take(ridge_blocks, tile_rows, axis=0)[:, None, :] * same[:, None, None]
    tiles = owned / divisor + diag

    p_rows = jnp.einsum("ipr,qr->ipq", col_rows, chol_inv, precision=HI)
    p_cols = jnp.einsum("ipr,qr->ipq", col_cols, chol_inv, precision=HI)
    row_ids = group * 8 + jnp.arange(8, dtype=jnp.int32)
    col_ids = jnp.arange(per_row, dtype=jnp.int32) * 8 + member
    p_rows = jnp.where((row_ids == 0)[:, None, None], chol[None], p_rows)
    p_cols = jnp.where((col_ids == 0)[:, None, None], chol[None], p_cols)

    update = jnp.einsum("apr,qsr->aqps", p_rows, p_cols, precision=HI)
    update = update.reshape(ACT * per_row, BLK, BLK)
    left_tiles = jnp.repeat(p_rows, per_row, axis=0)
    right_tiles = jnp.tile(p_cols, (ACT, 1, 1))
    trailing = ((tile_rows > 0) & (tile_cols > 0))[:, None, None]
    on_column = (tile_cols == 0)[:, None, None]
    on_row = ((tile_rows == 0) & (tile_cols > 0))[:, None, None]
    tiles = jnp.where(trailing, tiles - update, tiles)
    tiles = jnp.where(on_column, left_tiles, tiles)
    tiles = jnp.where(on_row, jnp.transpose(right_tiles, (0, 2, 1)), tiles)
    return tiles[None]


def solution(mesh):
    n_mem = mesh.shape["mem"]
    n_grp = mesh.shape["grp"]
    fast = n_mem == 8 and n_grp * 8 == NB
    body = on_device_fast if fast else on_device_general
    in_specs = (P(("grp", "mem"), None), P(("grp", "mem"), None), P())
    out_specs = P("mem", "grp", None, None)
    return jax.shard_map(
        body, mesh=mesh, in_specs=in_specs, out_specs=out_specs, check_vma=False
    )
```

```python
import jax
import jax.numpy as jnp
from jax import lax
from jax.sharding import PartitionSpec as P

NB = 32
BLK = 128
ACT = 8
HI = lax.Precision.HIGHEST


def panel_solve(column):
    count = column.shape[0]
    chol = jnp.linalg.cholesky(column[0])
    stacked = jnp.transpose(column, (2, 0, 1)).reshape(BLK, count * BLK)
    solved = lax.linalg.triangular_solve(chol, stacked, left_side=True, lower=True)
    lower_col = jnp.transpose(solved.reshape(BLK, count, BLK), (1, 2, 0))
    return lower_col.at[0].set(chol)


def apply_step(tiles, lower_col, step, tile_rows, tile_cols):
    left_tiles = jnp.take(lower_col, jnp.maximum(tile_rows - step, 0), axis=0)
    right_tiles = jnp.take(lower_col, jnp.maximum(tile_cols - step, 0), axis=0)
    update = jnp.einsum("tpr,tqr->tpq", left_tiles, right_tiles, precision=HI)
    trailing = ((tile_rows > step) & (tile_cols > step))[:, None, None]
    on_column = ((tile_cols == step) & (tile_rows >= step))[:, None, None]
    on_row = ((tile_rows == step) & (tile_cols > step))[:, None, None]
    tiles = jnp.where(trailing, tiles - update, tiles)
    tiles = jnp.where(on_column, left_tiles, tiles)
    tiles = jnp.where(on_row, jnp.transpose(right_tiles, (0, 2, 1)), tiles)
    return tiles


def column_picker(step, tile_rows, tile_cols):
    wanted = step + jnp.arange(NB - step, dtype=jnp.int32)
    inside = (tile_cols == step) & (tile_rows >= step)
    return ((tile_rows[None, :] == wanted[:, None]) & inside[None, :]).astype(jnp.float32)


def on_device_general(design, active_blocks, ridge):
    n_mem = lax.axis_size("mem")
    n_grp = lax.axis_size("grp")
    member = lax.axis_index("mem")
    group = lax.axis_index("grp")
    classes = n_mem // 8
    per_pos = ACT // classes
    per_row = NB // ACT
    slot_count = NB // classes * per_row
    owned_count = slot_count // n_grp
    row_count = design.shape[0]
    residue = member // 8
    position = member % 8
    everyone = lax.all_gather(active_blocks, "mem", axis=0, tiled=True)
    blocks = design.reshape(row_count, ACT, BLK)
    left = blocks.reshape(row_count, per_pos, classes, BLK)
    outgoing = jnp.einsum("ncqk,nbl->qbckl", left, blocks, preferred_element_type=jnp.float32)
    outgoing = outgoing.reshape(n_mem, per_pos, BLK, BLK)
    received = lax.all_to_all(outgoing, "mem", split_axis=0, concat_axis=0, tiled=True)
    row_ids = jnp.take(everyone.reshape(n_mem, per_pos, classes), residue, axis=2)
    col_ids = jnp.take(everyone, position, axis=1)
    targets = row_ids // classes * per_row + (col_ids // 8)[:, None]
    onehot = (
        targets.reshape(-1)[None, :] == jnp.arange(slot_count, dtype=jnp.int32)[:, None]
    ).astype(jnp.float32)
    sums = jnp.dot(
        onehot,
        received.reshape(n_mem * per_pos, BLK * BLK),
        precision=HI,
        preferred_element_type=jnp.float32,
    )
    sums = sums.reshape(slot_count, BLK, BLK)
    owned = lax.psum_scatter(sums, "grp", scatter_dimension=0, tiled=True)
    slots = group * owned_count + jnp.arange(owned_count, dtype=jnp.int32)
    tile_rows = slots // per_row * classes + residue
    tile_cols = slots % per_row * 8 + position
    ridge_blocks = jnp.take(ridge.reshape(NB, BLK), tile_rows, axis=0)
    same = (tile_rows == tile_cols).astype(jnp.float32)
    extra = jnp.eye(BLK, dtype=jnp.float32)[None] * ridge_blocks[:, None, :] * same[:, None, None]
    divisor = jnp.float32(row_count * n_grp * n_mem // 16)
    tiles = owned / divisor + extra
    picker = column_picker(0, tile_rows, tile_cols)
    partial_value = jnp.einsum("it,tpq->ipq", picker, tiles, precision=HI)
    column = lax.psum(partial_value, ("grp", "mem"))
    lower_col = panel_solve(column)
    tiles = apply_step(tiles, lower_col, 0, tile_rows, tile_cols)
    return tiles[None]


def on_device_fast(design, active_blocks, ridge):
    n_mem = lax.axis_size("mem")
    n_grp = lax.axis_size("grp")
    member = lax.axis_index("mem")
    group = lax.axis_index("grp")
    per_row = NB // ACT
    sizes = (2, 6)
    starts = (0, 2)
    row_count = design.shape[0]
    divisor = jnp.float32(row_count * n_grp * n_mem // 16)
    eye = jnp.eye(BLK, dtype=jnp.float32)
    ridge_blocks = ridge.reshape(NB, BLK)

    blocks = design.reshape(row_count, ACT, BLK)
    id_rows = jnp.zeros((8, BLK), jnp.float32).at[0, :ACT].set(active_blocks[0].astype(jnp.float32))
    id_rows = jnp.broadcast_to(id_rows[None, None], (n_mem, 1, 8, BLK))
    grp_ids = jnp.arange(n_grp, dtype=jnp.int32)
    q_ids = jnp.arange(per_row, dtype=jnp.int32)

    owned_parts = []
    prev = None
    for k in range(len(sizes)):
        per_chunk = sizes[k]
        lo = starts[k]
        pos_ids = jnp.arange(per_chunk, dtype=jnp.int32)
        piece = jnp.einsum(
            "nak,nbl->bakl", blocks[:, lo:lo + per_chunk], blocks, preferred_element_type=jnp.float32
        )
        if prev is not None:
            piece, prev = lax.optimization_barrier((piece, prev))
        else:
            ids_here = jnp.broadcast_to(id_rows, (n_mem, per_chunk, 8, BLK))
            piece = jnp.concatenate([piece, ids_here], axis=2)
        got_piece = lax.all_to_all(piece, "mem", split_axis=0, concat_axis=0, tiled=True)
        if prev is None:
            everyone = got_piece[:, 0, BLK, :ACT].astype(jnp.int32)
            got_piece = got_piece[:, :, :BLK]
            row_grp = everyone // 8
            col_grp = jnp.take(everyone, member, axis=1) // 8
            zero_on = everyone[:, 0] == 0
        got_piece = got_piece.reshape(n_mem, per_chunk, BLK, BLK)
        prev = got_piece
        rg = row_grp[:, lo:lo + per_chunk]
        sel = (
            (pos_ids[None, :, None, None, None] == pos_ids[None, None, None, None, :])
            & (rg[None, None, None, :, :] == grp_ids[:, None, None, None, None])
            & (col_grp[None, None, None, :, None] == q_ids[None, None, :, None, None])
        )
        sel = sel.reshape(n_grp, per_chunk * per_row, n_mem * per_chunk)
        if k == 0:
            first = pos_ids == 0
            col_sel = (
                (col_grp[None, :, None] == grp_ids[:, None, None])
                & zero_on[None, :, None]
                & first[None, None, :]
            ).reshape(n_grp, 1, n_mem * per_chunk)
            sel = jnp.concatenate([sel, col_sel], axis=1)
        width = sel.shape[1]
        send = jnp.dot(
            sel.reshape(n_grp * width, n_mem * per_chunk).astype(jnp.float32),
            got_piece.reshape(n_mem * per_chunk, BLK * BLK),
            precision=lax.Precision.HIGH,
            preferred_element_type=jnp.float32,
        ).reshape(n_grp * width, BLK, BLK)
        got = lax.psum_scatter(send, "grp", scatter_dimension=0, tiled=True)
        owned_parts.append(got[: per_chunk * per_row])
        if k == 0:
            col_tile = jnp.transpose(got[per_chunk * per_row]) / divisor
    owned = jnp.concatenate(owned_parts, axis=0)

    col_tile, prev = lax.optimization_barrier((col_tile, prev))
    spread = jnp.broadcast_to(col_tile[None], (n_grp, BLK, BLK))
    col_cols = lax.all_to_all(spread, "grp", split_axis=0, concat_axis=0, tiled=True)
    pair = jnp.broadcast_to(jnp.stack([col_tile, col_cols[0]])[None], (n_mem, 2, BLK, BLK))
    pairs = lax.all_to_all(pair, "mem", split_axis=0, concat_axis=0, tiled=True)
    col_rows = pairs[:, 0]
    a00 = pairs[0, 1] + eye * ridge_blocks[0][None, :]
    chol = jnp.linalg.cholesky(a00)
    chol_inv = lax.linalg.triangular_solve(chol, eye, left_side=True, lower=True)

    t = jnp.arange(ACT * per_row, dtype=jnp.int32)
    tile_rows = group * 8 + t // per_row
    tile_cols = (t % per_row) * 8 + member
    same = (tile_rows == tile_cols).astype(jnp.float32)
    diag = eye[None] * jnp.take(ridge_blocks, tile_rows, axis=0)[:, None, :] * same[:, None, None]
    tiles = owned / divisor + diag

    p_rows = jnp.einsum("ipr,qr->ipq", col_rows, chol_inv, precision=HI)
    p_cols = jnp.einsum("ipr,qr->ipq", col_cols, chol_inv, precision=HI)
    row_ids = group * 8 + jnp.arange(8, dtype=jnp.int32)
    col_ids = jnp.arange(per_row, dtype=jnp.int32) * 8 + member
    p_rows = jnp.where((row_ids == 0)[:, None, None], chol[None], p_rows)
    p_cols = jnp.where((col_ids == 0)[:, None, None], chol[None], p_cols)

    update = jnp.einsum("apr,qsr->aqps", p_rows, p_cols, precision=HI)
    update = update.reshape(ACT * per_row, BLK, BLK)
    left_tiles = jnp.repeat(p_rows, per_row, axis=0)
    right_tiles = jnp.tile(p_cols, (ACT, 1, 1))
    trailing = ((tile_rows > 0) & (tile_cols > 0))[:, None, None]
    on_column = (tile_cols == 0)[:, None, None]
    on_row = ((tile_rows == 0) & (tile_cols > 0))[:, None, None]
    tiles = jnp.where(trailing, tiles - update, tiles)
    tiles = jnp.where(on_column, left_tiles, tiles)
    tiles = jnp.where(on_row, jnp.transpose(right_tiles, (0, 2, 1)), tiles)
    return tiles[None]


def solution(mesh):
    n_mem = mesh.shape["mem"]
    n_grp = mesh.shape["grp"]
    fast = n_mem == 8 and n_grp * 8 == NB
    body = on_device_fast if fast else on_device_general
    in_specs = (P(("grp", "mem"), None), P(("grp", "mem"), None), P())
    out_specs = P("mem", "grp", None, None)
    return jax.shard_map(
        body, mesh=mesh, in_specs=in_specs, out_specs=out_specs, check_vma=False
    )
```

```python
import jax
import jax.numpy as jnp
from jax import lax
from jax.sharding import PartitionSpec as P

NB = 32
BLK = 128
ACT = 8
HI = lax.Precision.HIGHEST


def panel_solve(column):
    count = column.shape[0]
    chol = jnp.linalg.cholesky(column[0])
    stacked = jnp.transpose(column, (2, 0, 1)).reshape(BLK, count * BLK)
    solved = lax.linalg.triangular_solve(chol, stacked, left_side=True, lower=True)
    lower_col = jnp.transpose(solved.reshape(BLK, count, BLK), (1, 2, 0))
    return lower_col.at[0].set(chol)


def apply_step(tiles, lower_col, step, tile_rows, tile_cols):
    left_tiles = jnp.take(lower_col, jnp.maximum(tile_rows - step, 0), axis=0)
    right_tiles = jnp.take(lower_col, jnp.maximum(tile_cols - step, 0), axis=0)
    update = jnp.einsum("tpr,tqr->tpq", left_tiles, right_tiles, precision=HI)
    trailing = ((tile_rows > step) & (tile_cols > step))[:, None, None]
    on_column = ((tile_cols == step) & (tile_rows >= step))[:, None, None]
    on_row = ((tile_rows == step) & (tile_cols > step))[:, None, None]
    tiles = jnp.where(trailing, tiles - update, tiles)
    tiles = jnp.where(on_column, left_tiles, tiles)
    tiles = jnp.where(on_row, jnp.transpose(right_tiles, (0, 2, 1)), tiles)
    return tiles


def column_picker(step, tile_rows, tile_cols):
    wanted = step + jnp.arange(NB - step, dtype=jnp.int32)
    inside = (tile_cols == step) & (tile_rows >= step)
    return ((tile_rows[None, :] == wanted[:, None]) & inside[None, :]).astype(jnp.float32)


def on_device_general(design, active_blocks, ridge):
    n_mem = lax.axis_size("mem")
    n_grp = lax.axis_size("grp")
    member = lax.axis_index("mem")
    group = lax.axis_index("grp")
    classes = n_mem // 8
    per_pos = ACT // classes
    per_row = NB // ACT
    slot_count = NB // classes * per_row
    owned_count = slot_count // n_grp
    row_count = design.shape[0]
    residue = member // 8
    position = member % 8
    everyone = lax.all_gather(active_blocks, "mem", axis=0, tiled=True)
    blocks = design.reshape(row_count, ACT, BLK)
    left = blocks.reshape(row_count, per_pos, classes, BLK)
    outgoing = jnp.einsum("ncqk,nbl->qbckl", left, blocks, preferred_element_type=jnp.float32)
    outgoing = outgoing.reshape(n_mem, per_pos, BLK, BLK)
    received = lax.all_to_all(outgoing, "mem", split_axis=0, concat_axis=0, tiled=True)
    row_ids = jnp.take(everyone.reshape(n_mem, per_pos, classes), residue, axis=2)
    col_ids = jnp.take(everyone, position, axis=1)
    targets = row_ids // classes * per_row + (col_ids // 8)[:, None]
    onehot = (
        targets.reshape(-1)[None, :] == jnp.arange(slot_count, dtype=jnp.int32)[:, None]
    ).astype(jnp.float32)
    sums = jnp.dot(
        onehot,
        received.reshape(n_mem * per_pos, BLK * BLK),
        precision=HI,
        preferred_element_type=jnp.float32,
    )
    sums = sums.reshape(slot_count, BLK, BLK)
    owned = lax.psum_scatter(sums, "grp", scatter_dimension=0, tiled=True)
    slots = group * owned_count + jnp.arange(owned_count, dtype=jnp.int32)
    tile_rows = slots // per_row * classes + residue
    tile_cols = slots % per_row * 8 + position
    ridge_blocks = jnp.take(ridge.reshape(NB, BLK), tile_rows, axis=0)
    same = (tile_rows == tile_cols).astype(jnp.float32)
    extra = jnp.eye(BLK, dtype=jnp.float32)[None] * ridge_blocks[:, None, :] * same[:, None, None]
    divisor = jnp.float32(row_count * n_grp * n_mem // 16)
    tiles = owned / divisor + extra
    picker = column_picker(0, tile_rows, tile_cols)
    partial_value = jnp.einsum("it,tpq->ipq", picker, tiles, precision=HI)
    column = lax.psum(partial_value, ("grp", "mem"))
    lower_col = panel_solve(column)
    tiles = apply_step(tiles, lower_col, 0, tile_rows, tile_cols)
    return tiles[None]


def on_device_fast(design, active_blocks, ridge):
    n_mem = lax.axis_size("mem")
    n_grp = lax.axis_size("grp")
    member = lax.axis_index("mem")
    group = lax.axis_index("grp")
    per_row = NB // ACT
    sizes = (1, 2, 5)
    starts = (0, 1, 3)
    row_count = design.shape[0]
    divisor = jnp.float32(row_count * n_grp * n_mem // 16)
    eye = jnp.eye(BLK, dtype=jnp.float32)
    ridge_blocks = ridge.reshape(NB, BLK)

    blocks = design.reshape(row_count, ACT, BLK)
    id_rows = jnp.zeros((8, BLK), jnp.float32).at[0, :ACT].set(active_blocks[0].astype(jnp.float32))
    id_rows = jnp.broadcast_to(id_rows[None, None], (n_mem, 1, 8, BLK))
    grp_ids = jnp.arange(n_grp, dtype=jnp.int32)
    q_ids = jnp.arange(per_row, dtype=jnp.int32)

    owned_parts = []
    prev = None
    for k in range(len(sizes)):
        per_chunk = sizes[k]
        lo = starts[k]
        pos_ids = jnp.arange(per_chunk, dtype=jnp.int32)
        piece = jnp.einsum(
            "nak,nbl->bakl", blocks[:, lo:lo + per_chunk], blocks, preferred_element_type=jnp.float32
        )
        if prev is not None:
            piece, prev = lax.optimization_barrier((piece, prev))
        else:
            ids_here = jnp.broadcast_to(id_rows, (n_mem, per_chunk, 8, BLK))
            piece = jnp.concatenate([piece, ids_here], axis=2)
        got_piece = lax.all_to_all(piece, "mem", split_axis=0, concat_axis=0, tiled=True)
        if prev is None:
            everyone = got_piece[:, 0, BLK, :ACT].astype(jnp.int32)
            got_piece = got_piece[:, :, :BLK]
            row_grp = everyone // 8
            col_grp = jnp.take(everyone, member, axis=1) // 8
            zero_on = everyone[:, 0] == 0
        got_piece = got_piece.reshape(n_mem, per_chunk, BLK, BLK)
        prev = got_piece
        rg = row_grp[:, lo:lo + per_chunk]
        sel = (
            (pos_ids[None, :, None, None, None] == pos_ids[None, None, None, None, :])
            & (rg[None, None, None, :, :] == grp_ids[:, None, None, None, None])
            & (col_grp[None, None, None, :, None] == q_ids[None, None, :, None, None])
        )
        sel = sel.reshape(n_grp, per_chunk * per_row, n_mem * per_chunk)
        if k == 0:
            first = pos_ids == 0
            col_sel = (
                (col_grp[None, :, None] == grp_ids[:, None, None])
                & zero_on[None, :, None]
                & first[None, None, :]
            ).reshape(n_grp, 1, n_mem * per_chunk)
            sel = jnp.concatenate([sel, col_sel], axis=1)
        width = sel.shape[1]
        send = jnp.dot(
            sel.reshape(n_grp * width, n_mem * per_chunk).astype(jnp.float32),
            got_piece.reshape(n_mem * per_chunk, BLK * BLK),
            precision=lax.Precision.HIGH,
            preferred_element_type=jnp.float32,
        ).reshape(n_grp * width, BLK, BLK)
        got = lax.psum_scatter(send, "grp", scatter_dimension=0, tiled=True)
        owned_parts.append(got[: per_chunk * per_row])
        if k == 0:
            col_tile = jnp.transpose(got[per_chunk * per_row]) / divisor
    owned = jnp.concatenate(owned_parts, axis=0)

    col_tile, prev = lax.optimization_barrier((col_tile, prev))
    spread = jnp.broadcast_to(col_tile[None], (n_grp, BLK, BLK))
    col_cols = lax.all_to_all(spread, "grp", split_axis=0, concat_axis=0, tiled=True)
    pair = jnp.broadcast_to(jnp.stack([col_tile, col_cols[0]])[None], (n_mem, 2, BLK, BLK))
    pairs = lax.all_to_all(pair, "mem", split_axis=0, concat_axis=0, tiled=True)
    col_rows = pairs[:, 0]
    a00 = pairs[0, 1] + eye * ridge_blocks[0][None, :]
    chol = jnp.linalg.cholesky(a00)
    chol_inv = lax.linalg.triangular_solve(chol, eye, left_side=True, lower=True)

    t = jnp.arange(ACT * per_row, dtype=jnp.int32)
    tile_rows = group * 8 + t // per_row
    tile_cols = (t % per_row) * 8 + member
    same = (tile_rows == tile_cols).astype(jnp.float32)
    diag = eye[None] * jnp.take(ridge_blocks, tile_rows, axis=0)[:, None, :] * same[:, None, None]
    tiles = owned / divisor + diag

    p_rows = jnp.einsum("ipr,qr->ipq", col_rows, chol_inv, precision=HI)
    p_cols = jnp.einsum("ipr,qr->ipq", col_cols, chol_inv, precision=HI)
    row_ids = group * 8 + jnp.arange(8, dtype=jnp.int32)
    col_ids = jnp.arange(per_row, dtype=jnp.int32) * 8 + member
    p_rows = jnp.where((row_ids == 0)[:, None, None], chol[None], p_rows)
    p_cols = jnp.where((col_ids == 0)[:, None, None], chol[None], p_cols)

    update = jnp.einsum("apr,qsr->aqps", p_rows, p_cols, precision=HI)
    update = update.reshape(ACT * per_row, BLK, BLK)
    left_tiles = jnp.repeat(p_rows, per_row, axis=0)
    right_tiles = jnp.tile(p_cols, (ACT, 1, 1))
    trailing = ((tile_rows > 0) & (tile_cols > 0))[:, None, None]
    on_column = (tile_cols == 0)[:, None, None]
    on_row = ((tile_rows == 0) & (tile_cols > 0))[:, None, None]
    tiles = jnp.where(trailing, tiles - update, tiles)
    tiles = jnp.where(on_column, left_tiles, tiles)
    tiles = jnp.where(on_row, jnp.transpose(right_tiles, (0, 2, 1)), tiles)
    return tiles[None]


def solution(mesh):
    n_mem = mesh.shape["mem"]
    n_grp = mesh.shape["grp"]
    fast = n_mem == 8 and n_grp * 8 == NB
    body = on_device_fast if fast else on_device_general
    in_specs = (P(("grp", "mem"), None), P(("grp", "mem"), None), P())
    out_specs = P("mem", "grp", None, None)
    return jax.shard_map(
        body, mesh=mesh, in_specs=in_specs, out_specs=out_specs, check_vma=False
    )
```

```python
import jax
import jax.numpy as jnp
from jax import lax
from jax.sharding import PartitionSpec as P

NB = 32
BLK = 128
ACT = 8
HI = lax.Precision.HIGHEST


def panel_solve(column):
    count = column.shape[0]
    chol = jnp.linalg.cholesky(column[0])
    stacked = jnp.transpose(column, (2, 0, 1)).reshape(BLK, count * BLK)
    solved = lax.linalg.triangular_solve(chol, stacked, left_side=True, lower=True)
    lower_col = jnp.transpose(solved.reshape(BLK, count, BLK), (1, 2, 0))
    return lower_col.at[0].set(chol)


def apply_step(tiles, lower_col, step, tile_rows, tile_cols):
    left_tiles = jnp.take(lower_col, jnp.maximum(tile_rows - step, 0), axis=0)
    right_tiles = jnp.take(lower_col, jnp.maximum(tile_cols - step, 0), axis=0)
    update = jnp.einsum("tpr,tqr->tpq", left_tiles, right_tiles, precision=HI)
    trailing = ((tile_rows > step) & (tile_cols > step))[:, None, None]
    on_column = ((tile_cols == step) & (tile_rows >= step))[:, None, None]
    on_row = ((tile_rows == step) & (tile_cols > step))[:, None, None]
    tiles = jnp.where(trailing, tiles - update, tiles)
    tiles = jnp.where(on_column, left_tiles, tiles)
    tiles = jnp.where(on_row, jnp.transpose(right_tiles, (0, 2, 1)), tiles)
    return tiles


def column_picker(step, tile_rows, tile_cols):
    wanted = step + jnp.arange(NB - step, dtype=jnp.int32)
    inside = (tile_cols == step) & (tile_rows >= step)
    return ((tile_rows[None, :] == wanted[:, None]) & inside[None, :]).astype(jnp.float32)


def on_device_general(design, active_blocks, ridge):
    n_mem = lax.axis_size("mem")
    n_grp = lax.axis_size("grp")
    member = lax.axis_index("mem")
    group = lax.axis_index("grp")
    classes = n_mem // 8
    per_pos = ACT // classes
    per_row = NB // ACT
    slot_count = NB // classes * per_row
    owned_count = slot_count // n_grp
    row_count = design.shape[0]
    residue = member // 8
    position = member % 8
    everyone = lax.all_gather(active_blocks, "mem", axis=0, tiled=True)
    blocks = design.reshape(row_count, ACT, BLK)
    left = blocks.reshape(row_count, per_pos, classes, BLK)
    outgoing = jnp.einsum("ncqk,nbl->qbckl", left, blocks, preferred_element_type=jnp.float32)
    outgoing = outgoing.reshape(n_mem, per_pos, BLK, BLK)
    received = lax.all_to_all(outgoing, "mem", split_axis=0, concat_axis=0, tiled=True)
    row_ids = jnp.take(everyone.reshape(n_mem, per_pos, classes), residue, axis=2)
    col_ids = jnp.take(everyone, position, axis=1)
    targets = row_ids // classes * per_row + (col_ids // 8)[:, None]
    onehot = (
        targets.reshape(-1)[None, :] == jnp.arange(slot_count, dtype=jnp.int32)[:, None]
    ).astype(jnp.float32)
    sums = jnp.dot(
        onehot,
        received.reshape(n_mem * per_pos, BLK * BLK),
        precision=HI,
        preferred_element_type=jnp.float32,
    )
    sums = sums.reshape(slot_count, BLK, BLK)
    owned = lax.psum_scatter(sums, "grp", scatter_dimension=0, tiled=True)
    slots = group * owned_count + jnp.arange(owned_count, dtype=jnp.int32)
    tile_rows = slots // per_row * classes + residue
    tile_cols = slots % per_row * 8 + position
    ridge_blocks = jnp.take(ridge.reshape(NB, BLK), tile_rows, axis=0)
    same = (tile_rows == tile_cols).astype(jnp.float32)
    extra = jnp.eye(BLK, dtype=jnp.float32)[None] * ridge_blocks[:, None, :] * same[:, None, None]
    divisor = jnp.float32(row_count * n_grp * n_mem // 16)
    tiles = owned / divisor + extra
    picker = column_picker(0, tile_rows, tile_cols)
    partial_value = jnp.einsum("it,tpq->ipq", picker, tiles, precision=HI)
    column = lax.psum(partial_value, ("grp", "mem"))
    lower_col = panel_solve(column)
    tiles = apply_step(tiles, lower_col, 0, tile_rows, tile_cols)
    return tiles[None]


def on_device_fast(design, active_blocks, ridge):
    n_mem = lax.axis_size("mem")
    n_grp = lax.axis_size("grp")
    member = lax.axis_index("mem")
    group = lax.axis_index("grp")
    per_row = NB // ACT
    sizes = (1, 3, 4)
    starts = (0, 1, 4)
    tail = 5
    row_count = design.shape[0]
    divisor = jnp.float32(row_count * n_grp * n_mem // 16)
    eye = jnp.eye(BLK, dtype=jnp.float32)
    ridge_blocks = ridge.reshape(NB, BLK)

    blocks = design.reshape(row_count, ACT, BLK)
    id_rows = jnp.zeros((8, BLK), jnp.float32).at[0, :ACT].set(active_blocks[0].astype(jnp.float32))
    id_rows = jnp.broadcast_to(id_rows[None, None], (n_mem, 1, 8, BLK))
    grp_ids = jnp.arange(n_grp, dtype=jnp.int32)
    q_ids = jnp.arange(per_row, dtype=jnp.int32)

    by_d = {}
    prev = None
    for k in range(len(sizes)):
        per_chunk = sizes[k]
        lo = starts[k]
        pos_ids = jnp.arange(per_chunk, dtype=jnp.int32)
        rows_at = [[(b + lo + dl) % ACT for dl in range(per_chunk)] for b in range(n_mem)]
        left = blocks[:, jnp.array(rows_at, dtype=jnp.int32)]
        piece = jnp.einsum("nbdk,nbl->bdkl", left, blocks, preferred_element_type=jnp.float32)
        if k == 0:
            row0 = jnp.einsum("nk,nbl->bkl", blocks[:, 0], blocks, preferred_element_type=jnp.float32)
            piece = jnp.concatenate([piece, row0[:, None]], axis=1)
        if prev is not None:
            piece, prev = lax.optimization_barrier((piece, prev))
        else:
            ids_here = jnp.broadcast_to(id_rows, (n_mem, piece.shape[1], 8, BLK))
            piece = jnp.concatenate([piece, ids_here], axis=2)
        got_piece = lax.all_to_all(piece, "mem", split_axis=0, concat_axis=0, tiled=True)
        if prev is None:
            everyone = got_piece[:, 0, BLK, :ACT].astype(jnp.int32)
            got_piece = got_piece[:, :, :BLK]
            row_grp = everyone // 8
            col_grp = jnp.take(everyone, member, axis=1) // 8
            zero_on = everyone[:, 0] == 0
        if k == 0:
            row0_got = got_piece[:, per_chunk]
            got_piece = got_piece[:, :per_chunk]
        prev = got_piece
        flat = got_piece.reshape(n_mem * per_chunk, BLK * BLK)
        apos = (member + lo + pos_ids) % ACT
        rg = jnp.take(row_grp, apos, axis=1)
        sel = (
            (pos_ids[None, :, None, None, None] == pos_ids[None, None, None, None, :])
            & (rg[None, None, None, :, :] == grp_ids[:, None, None, None, None])
            & (col_grp[None, None, None, :, None] == q_ids[None, None, :, None, None])
        )
        keep = [
            [(dl, q) for dl in range(per_chunk) for q in range(per_row) if not (lo + dl >= tail and q == g)]
            for g in range(n_grp)
        ]
        sel = jnp.stack([jnp.stack([sel[g, dl, q] for dl, q in keep[g]]) for g in range(n_grp)])
        kept_rows = sel.shape[1]
        if k == 0:
            col_sel = (
                (col_grp[None, :] == grp_ids[:, None]) & zero_on[None, :]
            ).astype(jnp.float32)
            col_part = jnp.dot(
                col_sel, row0_got.reshape(n_mem, BLK * BLK), precision=HI,
                preferred_element_type=jnp.float32,
            ).reshape(n_grp, 1, BLK * BLK)
        send = jnp.dot(
            sel.reshape(n_grp * kept_rows, n_mem * per_chunk).astype(jnp.float32),
            flat,
            precision=lax.Precision.HIGH,
            preferred_element_type=jnp.float32,
        ).reshape(n_grp, kept_rows, BLK * BLK)
        if k == 0:
            send = jnp.concatenate([send, col_part], axis=1)
        width = send.shape[1]
        got = lax.psum_scatter(
            send.reshape(n_grp * width, BLK, BLK), "grp", scatter_dimension=0, tiled=True
        )
        if k == 0:
            col_tile = jnp.transpose(got[kept_rows]) / divisor
            got = got[:kept_rows]
        pos = 0
        for dl in range(per_chunk):
            width_d = per_row - 1 if lo + dl >= tail else per_row
            by_d[lo + dl] = got[pos:pos + width_d]
            pos += width_d

    for d in range(tail, ACT):
        shift = ACT - d
        src_tile = jnp.transpose(jnp.take(by_d[shift], group, axis=0))
        moved = lax.ppermute(
            src_tile, "mem", perm=[(j, (j + shift) % n_mem) for j in range(n_mem)]
        )
        others = by_d[d]
        slots = []
        for q in range(per_row):
            below = others[min(q, per_row - 2)]
            above = others[max(q - 1, 0)]
            slots.append(jnp.where(q == group, moved, jnp.where(q < group, below, above)))
        by_d[d] = jnp.stack(slots)
    owned = jnp.stack([by_d[d] for d in range(ACT)]).reshape(ACT * per_row, BLK, BLK)

    col_tile, prev = lax.optimization_barrier((col_tile, prev))
    spread = jnp.broadcast_to(col_tile[None], (n_grp, BLK, BLK))
    col_cols = lax.all_to_all(spread, "grp", split_axis=0, concat_axis=0, tiled=True)
    pair = jnp.broadcast_to(jnp.stack([col_tile, col_cols[0]])[None], (n_mem, 2, BLK, BLK))
    pairs = lax.all_to_all(pair, "mem", split_axis=0, concat_axis=0, tiled=True)
    col_rows = pairs[:, 0]
    a00 = pairs[0, 1] + eye * ridge_blocks[0][None, :]
    chol = jnp.linalg.cholesky(a00)
    chol_inv = lax.linalg.triangular_solve(chol, eye, left_side=True, lower=True)

    a_of_d = (member + jnp.arange(ACT, dtype=jnp.int32)) % ACT
    t = jnp.arange(ACT * per_row, dtype=jnp.int32)
    tile_rows = group * 8 + jnp.take(a_of_d, t // per_row)
    tile_cols = (t % per_row) * 8 + member
    same = (tile_rows == tile_cols).astype(jnp.float32)
    diag = eye[None] * jnp.take(ridge_blocks, tile_rows, axis=0)[:, None, :] * same[:, None, None]
    tiles = owned / divisor + diag

    p_rows = jnp.einsum("ipr,qr->ipq", col_rows, chol_inv, precision=HI)
    p_cols = jnp.einsum("ipr,qr->ipq", col_cols, chol_inv, precision=HI)
    p_rows = jnp.take(p_rows, a_of_d, axis=0)
    row_ids = group * 8 + a_of_d
    col_ids = jnp.arange(per_row, dtype=jnp.int32) * 8 + member
    p_rows = jnp.where((row_ids == 0)[:, None, None], chol[None], p_rows)
    p_cols = jnp.where((col_ids == 0)[:, None, None], chol[None], p_cols)

    update = jnp.einsum("apr,qsr->aqps", p_rows, p_cols, precision=HI)
    update = update.reshape(ACT * per_row, BLK, BLK)
    left_tiles = jnp.repeat(p_rows, per_row, axis=0)
    right_tiles = jnp.tile(p_cols, (ACT, 1, 1))
    trailing = ((tile_rows > 0) & (tile_cols > 0))[:, None, None]
    on_column = (tile_cols == 0)[:, None, None]
    on_row = ((tile_rows == 0) & (tile_cols > 0))[:, None, None]
    tiles = jnp.where(trailing, tiles - update, tiles)
    tiles = jnp.where(on_column, left_tiles, tiles)
    tiles = jnp.where(on_row, jnp.transpose(right_tiles, (0, 2, 1)), tiles)
    tiles = jnp.roll(tiles.reshape(ACT, per_row, BLK, BLK), member, axis=0)
    return tiles.reshape(1, ACT * per_row, BLK, BLK)


def solution(mesh):
    n_mem = mesh.shape["mem"]
    n_grp = mesh.shape["grp"]
    fast = n_mem == 8 and n_grp * 8 == NB
    body = on_device_fast if fast else on_device_general
    in_specs = (P(("grp", "mem"), None), P(("grp", "mem"), None), P())
    out_specs = P("mem", "grp", None, None)
    return jax.shard_map(
        body, mesh=mesh, in_specs=in_specs, out_specs=out_specs, check_vma=False
    )
```

```python
import jax
import jax.numpy as jnp
from jax import lax
from jax.sharding import PartitionSpec as P

NB = 32
BLK = 128
ACT = 8
HI = lax.Precision.HIGHEST


def panel_solve(column):
    count = column.shape[0]
    chol = jnp.linalg.cholesky(column[0])
    stacked = jnp.transpose(column, (2, 0, 1)).reshape(BLK, count * BLK)
    solved = lax.linalg.triangular_solve(chol, stacked, left_side=True, lower=True)
    lower_col = jnp.transpose(solved.reshape(BLK, count, BLK), (1, 2, 0))
    return lower_col.at[0].set(chol)


def apply_step(tiles, lower_col, step, tile_rows, tile_cols):
    left_tiles = jnp.take(lower_col, jnp.maximum(tile_rows - step, 0), axis=0)
    right_tiles = jnp.take(lower_col, jnp.maximum(tile_cols - step, 0), axis=0)
    update = jnp.einsum("tpr,tqr->tpq", left_tiles, right_tiles, precision=HI)
    trailing = ((tile_rows > step) & (tile_cols > step))[:, None, None]
    on_column = ((tile_cols == step) & (tile_rows >= step))[:, None, None]
    on_row = ((tile_rows == step) & (tile_cols > step))[:, None, None]
    tiles = jnp.where(trailing, tiles - update, tiles)
    tiles = jnp.where(on_column, left_tiles, tiles)
    tiles = jnp.where(on_row, jnp.transpose(right_tiles, (0, 2, 1)), tiles)
    return tiles


def column_picker(step, tile_rows, tile_cols):
    wanted = step + jnp.arange(NB - step, dtype=jnp.int32)
    inside = (tile_cols == step) & (tile_rows >= step)
    return ((tile_rows[None, :] == wanted[:, None]) & inside[None, :]).astype(jnp.float32)


def on_device_general(design, active_blocks, ridge):
    n_mem = lax.axis_size("mem")
    n_grp = lax.axis_size("grp")
    member = lax.axis_index("mem")
    group = lax.axis_index("grp")
    classes = n_mem // 8
    per_pos = ACT // classes
    per_row = NB // ACT
    slot_count = NB // classes * per_row
    owned_count = slot_count // n_grp
    row_count = design.shape[0]
    residue = member // 8
    position = member % 8
    everyone = lax.all_gather(active_blocks, "mem", axis=0, tiled=True)
    blocks = design.reshape(row_count, ACT, BLK)
    left = blocks.reshape(row_count, per_pos, classes, BLK)
    outgoing = jnp.einsum("ncqk,nbl->qbckl", left, blocks, preferred_element_type=jnp.float32)
    outgoing = outgoing.reshape(n_mem, per_pos, BLK, BLK)
    received = lax.all_to_all(outgoing, "mem", split_axis=0, concat_axis=0, tiled=True)
    row_ids = jnp.take(everyone.reshape(n_mem, per_pos, classes), residue, axis=2)
    col_ids = jnp.take(everyone, position, axis=1)
    targets = row_ids // classes * per_row + (col_ids // 8)[:, None]
    onehot = (
        targets.reshape(-1)[None, :] == jnp.arange(slot_count, dtype=jnp.int32)[:, None]
    ).astype(jnp.float32)
    sums = jnp.dot(
        onehot,
        received.reshape(n_mem * per_pos, BLK * BLK),
        precision=HI,
        preferred_element_type=jnp.float32,
    )
    sums = sums.reshape(slot_count, BLK, BLK)
    owned = lax.psum_scatter(sums, "grp", scatter_dimension=0, tiled=True)
    slots = group * owned_count + jnp.arange(owned_count, dtype=jnp.int32)
    tile_rows = slots // per_row * classes + residue
    tile_cols = slots % per_row * 8 + position
    ridge_blocks = jnp.take(ridge.reshape(NB, BLK), tile_rows, axis=0)
    same = (tile_rows == tile_cols).astype(jnp.float32)
    extra = jnp.eye(BLK, dtype=jnp.float32)[None] * ridge_blocks[:, None, :] * same[:, None, None]
    divisor = jnp.float32(row_count * n_grp * n_mem // 16)
    tiles = owned / divisor + extra
    picker = column_picker(0, tile_rows, tile_cols)
    partial_value = jnp.einsum("it,tpq->ipq", picker, tiles, precision=HI)
    column = lax.psum(partial_value, ("grp", "mem"))
    lower_col = panel_solve(column)
    tiles = apply_step(tiles, lower_col, 0, tile_rows, tile_cols)
    return tiles[None]


def on_device_fast(design, active_blocks, ridge):
    n_mem = lax.axis_size("mem")
    n_grp = lax.axis_size("grp")
    member = lax.axis_index("mem")
    group = lax.axis_index("grp")
    per_row = NB // ACT
    sizes = (1, 2, 5)
    starts = (0, 1, 3)
    row_count = design.shape[0]
    divisor = jnp.float32(row_count * n_grp * n_mem // 16)
    eye = jnp.eye(BLK, dtype=jnp.float32)
    ridge_blocks = ridge.reshape(NB, BLK)

    blocks = design.reshape(row_count, ACT, BLK)
    id_rows = jnp.zeros((8, BLK), jnp.float32).at[0, :ACT].set(active_blocks[0].astype(jnp.float32))
    id_rows = jnp.broadcast_to(id_rows[None, None], (n_mem, 1, 8, BLK))
    grp_ids = jnp.arange(n_grp, dtype=jnp.int32)
    q_ids = jnp.arange(per_row, dtype=jnp.int32)

    owned_parts = []
    prev = None
    for k in range(len(sizes)):
        per_chunk = sizes[k]
        lo = starts[k]
        pos_ids = jnp.arange(per_chunk, dtype=jnp.int32)
        piece = jnp.einsum(
            "nak,nbl->bakl", blocks[:, lo:lo + per_chunk], blocks, preferred_element_type=jnp.float32
        )
        if prev is not None:
            piece, prev = lax.optimization_barrier((piece, prev))
        else:
            ids_here = jnp.broadcast_to(id_rows, (n_mem, per_chunk, 8, BLK))
            piece = jnp.concatenate([piece, ids_here], axis=2)
        got_piece = lax.all_to_all(piece, "mem", split_axis=0, concat_axis=0, tiled=True)
        if prev is None:
            everyone = got_piece[:, 0, BLK, :ACT].astype(jnp.int32)
            got_piece = got_piece[:, :, :BLK]
            row_grp = everyone // 8
            col_grp = jnp.take(everyone, member, axis=1) // 8
            zero_on = everyone[:, 0] == 0
        got_piece = got_piece.reshape(n_mem, per_chunk, BLK, BLK)
        prev = got_piece
        rg = row_grp[:, lo:lo + per_chunk]
        sel = (
            (pos_ids[None, :, None, None, None] == pos_ids[None, None, None, None, :])
            & (rg[None, None, None, :, :] == grp_ids[:, None, None, None, None])
            & (col_grp[None, None, None, :, None] == q_ids[None, None, :, None, None])
        )
        sel = sel.reshape(n_grp, per_chunk * per_row, n_mem * per_chunk)
        if k == 0:
            first = pos_ids == 0
            col_sel = (
                (col_grp[None, :, None] == grp_ids[:, None, None])
                & zero_on[None, :, None]
                & first[None, None, :]
            ).reshape(n_grp, 1, n_mem * per_chunk)
            sel = jnp.concatenate([sel, col_sel], axis=1)
        width = sel.shape[1]
        send = jnp.dot(
            sel.reshape(n_grp * width, n_mem * per_chunk).astype(jnp.float32),
            got_piece.reshape(n_mem * per_chunk, BLK * BLK),
            precision=lax.Precision.HIGH,
            preferred_element_type=jnp.float32,
        ).reshape(n_grp * width, BLK, BLK)
        got = lax.psum_scatter(send, "grp", scatter_dimension=0, tiled=True)
        owned_parts.append(got[: per_chunk * per_row])
        if k == 0:
            col_tile = jnp.transpose(got[per_chunk * per_row]) / divisor
    owned = jnp.concatenate(owned_parts, axis=0)

    col_tile, prev = lax.optimization_barrier((col_tile, prev))
    spread = jnp.broadcast_to(col_tile[None], (n_grp, BLK, BLK))
    col_cols = lax.all_to_all(spread, "grp", split_axis=0, concat_axis=0, tiled=True)
    pair = jnp.broadcast_to(jnp.stack([col_tile, col_cols[0]])[None], (n_mem, 2, BLK, BLK))
    pairs = lax.all_to_all(pair, "mem", split_axis=0, concat_axis=0, tiled=True)
    col_rows = pairs[:, 0]
    a00 = pairs[0, 1] + eye * ridge_blocks[0][None, :]
    chol = jnp.linalg.cholesky(a00)
    chol_inv = lax.linalg.triangular_solve(chol, eye, left_side=True, lower=True)

    t = jnp.arange(ACT * per_row, dtype=jnp.int32)
    tile_rows = group * 8 + t // per_row
    tile_cols = (t % per_row) * 8 + member
    same = (tile_rows == tile_cols).astype(jnp.float32)
    diag = eye[None] * jnp.take(ridge_blocks, tile_rows, axis=0)[:, None, :] * same[:, None, None]

    p_rows = jnp.einsum("ipr,qr->ipq", col_rows, chol_inv, precision=HI)
    p_cols = jnp.einsum("ipr,qr->ipq", col_cols, chol_inv, precision=HI)
    row_ids = group * 8 + jnp.arange(8, dtype=jnp.int32)
    col_ids = jnp.arange(per_row, dtype=jnp.int32) * 8 + member
    p_rows = jnp.where((row_ids == 0)[:, None, None], chol[None], p_rows)
    p_cols = jnp.where((col_ids == 0)[:, None, None], chol[None], p_cols)

    update = jnp.einsum("apr,qsr->aqps", p_rows, p_cols, precision=HI)
    update = update.reshape(ACT * per_row, BLK, BLK)
    left_tiles = jnp.repeat(p_rows, per_row, axis=0)
    right_tiles = jnp.tile(p_cols, (ACT, 1, 1))
    trailing = ((tile_rows > 0) & (tile_cols > 0))[:, None, None]
    on_column = (tile_cols == 0)[:, None, None]
    on_row = ((tile_rows == 0) & (tile_cols > 0))[:, None, None]
    flipped = jnp.transpose(right_tiles, (0, 2, 1))

    def finish(lo, hi, part):
        piece = part / divisor + diag[lo:hi]
        piece = jnp.where(trailing[lo:hi], piece - update[lo:hi], piece)
        piece = jnp.where(on_column[lo:hi], left_tiles[lo:hi], piece)
        return jnp.where(on_row[lo:hi], flipped[lo:hi], piece)

    done = []
    first = 0
    for part in owned_parts:
        done.append(finish(first, first + part.shape[0], part))
        first += part.shape[0]
    early = lax.optimization_barrier(jnp.concatenate(done[:-1], axis=0))
    tiles = jnp.concatenate([early, done[-1]], axis=0)
    return tiles[None]


def solution(mesh):
    n_mem = mesh.shape["mem"]
    n_grp = mesh.shape["grp"]
    fast = n_mem == 8 and n_grp * 8 == NB
    body = on_device_fast if fast else on_device_general
    in_specs = (P(("grp", "mem"), None), P(("grp", "mem"), None), P())
    out_specs = P("mem", "grp", None, None)
    return jax.shard_map(
        body, mesh=mesh, in_specs=in_specs, out_specs=out_specs, check_vma=False
    )
```

```python
import jax
import jax.numpy as jnp
from jax import lax
from jax.sharding import PartitionSpec as P

NB = 32
BLK = 128
ACT = 8
HI = lax.Precision.HIGHEST


def panel_solve(column):
    count = column.shape[0]
    chol = jnp.linalg.cholesky(column[0])
    stacked = jnp.transpose(column, (2, 0, 1)).reshape(BLK, count * BLK)
    solved = lax.linalg.triangular_solve(chol, stacked, left_side=True, lower=True)
    lower_col = jnp.transpose(solved.reshape(BLK, count, BLK), (1, 2, 0))
    return lower_col.at[0].set(chol)


def apply_step(tiles, lower_col, step, tile_rows, tile_cols):
    left_tiles = jnp.take(lower_col, jnp.maximum(tile_rows - step, 0), axis=0)
    right_tiles = jnp.take(lower_col, jnp.maximum(tile_cols - step, 0), axis=0)
    update = jnp.einsum("tpr,tqr->tpq", left_tiles, right_tiles, precision=HI)
    trailing = ((tile_rows > step) & (tile_cols > step))[:, None, None]
    on_column = ((tile_cols == step) & (tile_rows >= step))[:, None, None]
    on_row = ((tile_rows == step) & (tile_cols > step))[:, None, None]
    tiles = jnp.where(trailing, tiles - update, tiles)
    tiles = jnp.where(on_column, left_tiles, tiles)
    tiles = jnp.where(on_row, jnp.transpose(right_tiles, (0, 2, 1)), tiles)
    return tiles


def column_picker(step, tile_rows, tile_cols):
    wanted = step + jnp.arange(NB - step, dtype=jnp.int32)
    inside = (tile_cols == step) & (tile_rows >= step)
    return ((tile_rows[None, :] == wanted[:, None]) & inside[None, :]).astype(jnp.float32)


def on_device_general(design, active_blocks, ridge):
    n_mem = lax.axis_size("mem")
    n_grp = lax.axis_size("grp")
    member = lax.axis_index("mem")
    group = lax.axis_index("grp")
    classes = n_mem // 8
    per_pos = ACT // classes
    per_row = NB // ACT
    slot_count = NB // classes * per_row
    owned_count = slot_count // n_grp
    row_count = design.shape[0]
    residue = member // 8
    position = member % 8
    everyone = lax.all_gather(active_blocks, "mem", axis=0, tiled=True)
    blocks = design.reshape(row_count, ACT, BLK)
    left = blocks.reshape(row_count, per_pos, classes, BLK)
    outgoing = jnp.einsum("ncqk,nbl->qbckl", left, blocks, preferred_element_type=jnp.float32)
    outgoing = outgoing.reshape(n_mem, per_pos, BLK, BLK)
    received = lax.all_to_all(outgoing, "mem", split_axis=0, concat_axis=0, tiled=True)
    row_ids = jnp.take(everyone.reshape(n_mem, per_pos, classes), residue, axis=2)
    col_ids = jnp.take(everyone, position, axis=1)
    targets = row_ids // classes * per_row + (col_ids // 8)[:, None]
    onehot = (
        targets.reshape(-1)[None, :] == jnp.arange(slot_count, dtype=jnp.int32)[:, None]
    ).astype(jnp.float32)
    sums = jnp.dot(
        onehot,
        received.reshape(n_mem * per_pos, BLK * BLK),
        precision=HI,
        preferred_element_type=jnp.float32,
    )
    sums = sums.reshape(slot_count, BLK, BLK)
    owned = lax.psum_scatter(sums, "grp", scatter_dimension=0, tiled=True)
    slots = group * owned_count + jnp.arange(owned_count, dtype=jnp.int32)
    tile_rows = slots // per_row * classes + residue
    tile_cols = slots % per_row * 8 + position
    ridge_blocks = jnp.take(ridge.reshape(NB, BLK), tile_rows, axis=0)
    same = (tile_rows == tile_cols).astype(jnp.float32)
    extra = jnp.eye(BLK, dtype=jnp.float32)[None] * ridge_blocks[:, None, :] * same[:, None, None]
    divisor = jnp.float32(row_count * n_grp * n_mem // 16)
    tiles = owned / divisor + extra
    picker = column_picker(0, tile_rows, tile_cols)
    partial_value = jnp.einsum("it,tpq->ipq", picker, tiles, precision=HI)
    column = lax.psum(partial_value, ("grp", "mem"))
    lower_col = panel_solve(column)
    tiles = apply_step(tiles, lower_col, 0, tile_rows, tile_cols)
    return tiles[None]


def on_device_fast(design, active_blocks, ridge):
    n_mem = lax.axis_size("mem")
    n_grp = lax.axis_size("grp")
    member = lax.axis_index("mem")
    group = lax.axis_index("grp")
    per_row = NB // ACT
    sizes = (1, 2, 5)
    starts = (0, 1, 3)
    row_count = design.shape[0]
    divisor = jnp.float32(row_count * n_grp * n_mem // 16)
    eye = jnp.eye(BLK, dtype=jnp.float32)
    ridge_blocks = ridge.reshape(NB, BLK)

    blocks = design.reshape(row_count, ACT, BLK)
    id_rows = jnp.zeros((8, BLK), jnp.float32).at[0, :ACT].set(active_blocks[0].astype(jnp.float32))
    id_rows = jnp.broadcast_to(id_rows[None, None], (n_mem, 1, 8, BLK))
    grp_ids = jnp.arange(n_grp, dtype=jnp.int32)
    q_ids = jnp.arange(per_row, dtype=jnp.int32)

    owned_parts = []
    prev = None
    for k in range(len(sizes)):
        per_chunk = sizes[k]
        lo = starts[k]
        pos_ids = jnp.arange(per_chunk, dtype=jnp.int32)
        piece = jnp.einsum(
            "nak,nbl->bakl", blocks[:, lo:lo + per_chunk], blocks, preferred_element_type=jnp.float32
        )
        if prev is not None:
            piece, prev = lax.optimization_barrier((piece, prev))
        else:
            ids_here = jnp.broadcast_to(id_rows, (n_mem, per_chunk, 8, BLK))
            piece = jnp.concatenate([piece, ids_here], axis=2)
        got_piece = lax.all_to_all(piece, "mem", split_axis=0, concat_axis=0, tiled=True)
        if prev is None:
            everyone = got_piece[:, 0, BLK, :ACT].astype(jnp.int32)
            got_piece = got_piece[:, :, :BLK]
            row_grp = everyone // 8
            col_grp = jnp.take(everyone, member, axis=1) // 8
            zero_on = everyone[:, 0] == 0
        got_piece = got_piece.reshape(n_mem, per_chunk, BLK, BLK)
        prev = got_piece
        rg = row_grp[:, lo:lo + per_chunk]
        sel = (
            (pos_ids[None, :, None, None, None] == pos_ids[None, None, None, None, :])
            & (rg[None, None, None, :, :] == grp_ids[:, None, None, None, None])
            & (col_grp[None, None, None, :, None] == q_ids[None, None, :, None, None])
        )
        sel = sel.reshape(n_grp, per_chunk * per_row, n_mem * per_chunk)
        if k == 0:
            first = pos_ids == 0
            col_sel = (
                (col_grp[None, :, None] == grp_ids[:, None, None])
                & zero_on[None, :, None]
                & first[None, None, :]
            ).reshape(n_grp, 1, n_mem * per_chunk)
            sel = jnp.concatenate([sel, col_sel], axis=1)
        width = sel.shape[1]
        send = jnp.dot(
            sel.reshape(n_grp * width, n_mem * per_chunk).astype(jnp.float32),
            got_piece.reshape(n_mem * per_chunk, BLK * BLK),
            precision=lax.Precision.HIGH,
            preferred_element_type=jnp.float32,
        ).reshape(n_grp * width, BLK, BLK)
        got = lax.psum_scatter(send, "grp", scatter_dimension=0, tiled=True)
        owned_parts.append(got[: per_chunk * per_row])
        if k == 0:
            col_tile = jnp.transpose(got[per_chunk * per_row]) / divisor
    owned = jnp.concatenate(owned_parts, axis=0)

    col_tile, prev = lax.optimization_barrier((col_tile, prev))
    spread = jnp.broadcast_to(col_tile[None], (n_grp, BLK, BLK))
    col_cols = lax.all_to_all(spread, "grp", split_axis=0, concat_axis=0, tiled=True)
    pair = jnp.broadcast_to(jnp.stack([col_tile, col_cols[0]])[None], (n_mem, 2, BLK, BLK))
    pairs = lax.all_to_all(pair, "mem", split_axis=0, concat_axis=0, tiled=True)
    col_rows = pairs[:, 0]
    a00 = pairs[0, 1] + eye * ridge_blocks[0][None, :]
    chol = jnp.linalg.cholesky(a00)
    chol_inv = lax.linalg.triangular_solve(chol, eye, left_side=True, lower=True)

    t = jnp.arange(ACT * per_row, dtype=jnp.int32)
    tile_rows = group * 8 + t // per_row
    tile_cols = (t % per_row) * 8 + member
    same = (tile_rows == tile_cols).astype(jnp.float32)
    diag = eye[None] * jnp.take(ridge_blocks, tile_rows, axis=0)[:, None, :] * same[:, None, None]

    p_rows = jnp.einsum("ipr,qr->ipq", col_rows, chol_inv, precision=HI)
    p_cols = jnp.einsum("ipr,qr->ipq", col_cols, chol_inv, precision=HI)
    row_ids = group * 8 + jnp.arange(8, dtype=jnp.int32)
    col_ids = jnp.arange(per_row, dtype=jnp.int32) * 8 + member
    p_rows = jnp.where((row_ids == 0)[:, None, None], chol[None], p_rows)
    p_cols = jnp.where((col_ids == 0)[:, None, None], chol[None], p_cols)

    update = jnp.einsum("apr,qsr->aqps", p_rows, p_cols, precision=HI)
    update = update.reshape(ACT * per_row, BLK, BLK)
    left_tiles = jnp.repeat(p_rows, per_row, axis=0)
    right_tiles = jnp.tile(p_cols, (ACT, 1, 1))
    trailing = ((tile_rows > 0) & (tile_cols > 0))[:, None, None]
    on_column = (tile_cols == 0)[:, None, None]
    on_row = ((tile_rows == 0) & (tile_cols > 0))[:, None, None]
    addend = jnp.where(trailing, diag - update, diag)
    replaced = on_column | on_row
    override = jnp.where(on_column, left_tiles, jnp.transpose(right_tiles, (0, 2, 1)))
    addend, override = lax.optimization_barrier((addend, override))
    tiles = jnp.where(replaced, override, owned / divisor + addend)
    return tiles[None]


def solution(mesh):
    n_mem = mesh.shape["mem"]
    n_grp = mesh.shape["grp"]
    fast = n_mem == 8 and n_grp * 8 == NB
    body = on_device_fast if fast else on_device_general
    in_specs = (P(("grp", "mem"), None), P(("grp", "mem"), None), P())
    out_specs = P("mem", "grp", None, None)
    return jax.shard_map(
        body, mesh=mesh, in_specs=in_specs, out_specs=out_specs, check_vma=False
    )
```

```python
import jax
import jax.numpy as jnp
from jax import lax
from jax.sharding import PartitionSpec as P

NB = 32
BLK = 128
ACT = 8
HI = lax.Precision.HIGHEST


def panel_solve(column):
    count = column.shape[0]
    chol = jnp.linalg.cholesky(column[0])
    stacked = jnp.transpose(column, (2, 0, 1)).reshape(BLK, count * BLK)
    solved = lax.linalg.triangular_solve(chol, stacked, left_side=True, lower=True)
    lower_col = jnp.transpose(solved.reshape(BLK, count, BLK), (1, 2, 0))
    return lower_col.at[0].set(chol)


def apply_step(tiles, lower_col, step, tile_rows, tile_cols):
    left_tiles = jnp.take(lower_col, jnp.maximum(tile_rows - step, 0), axis=0)
    right_tiles = jnp.take(lower_col, jnp.maximum(tile_cols - step, 0), axis=0)
    update = jnp.einsum("tpr,tqr->tpq", left_tiles, right_tiles, precision=HI)
    trailing = ((tile_rows > step) & (tile_cols > step))[:, None, None]
    on_column = ((tile_cols == step) & (tile_rows >= step))[:, None, None]
    on_row = ((tile_rows == step) & (tile_cols > step))[:, None, None]
    tiles = jnp.where(trailing, tiles - update, tiles)
    tiles = jnp.where(on_column, left_tiles, tiles)
    tiles = jnp.where(on_row, jnp.transpose(right_tiles, (0, 2, 1)), tiles)
    return tiles


def column_picker(step, tile_rows, tile_cols):
    wanted = step + jnp.arange(NB - step, dtype=jnp.int32)
    inside = (tile_cols == step) & (tile_rows >= step)
    return ((tile_rows[None, :] == wanted[:, None]) & inside[None, :]).astype(jnp.float32)


def on_device_general(design, active_blocks, ridge):
    n_mem = lax.axis_size("mem")
    n_grp = lax.axis_size("grp")
    member = lax.axis_index("mem")
    group = lax.axis_index("grp")
    classes = n_mem // 8
    per_pos = ACT // classes
    per_row = NB // ACT
    slot_count = NB // classes * per_row
    owned_count = slot_count // n_grp
    row_count = design.shape[0]
    residue = member // 8
    position = member % 8
    everyone = lax.all_gather(active_blocks, "mem", axis=0, tiled=True)
    blocks = design.reshape(row_count, ACT, BLK)
    left = blocks.reshape(row_count, per_pos, classes, BLK)
    outgoing = jnp.einsum("ncqk,nbl->qbckl", left, blocks, preferred_element_type=jnp.float32)
    outgoing = outgoing.reshape(n_mem, per_pos, BLK, BLK)
    received = lax.all_to_all(outgoing, "mem", split_axis=0, concat_axis=0, tiled=True)
    row_ids = jnp.take(everyone.reshape(n_mem, per_pos, classes), residue, axis=2)
    col_ids = jnp.take(everyone, position, axis=1)
    targets = row_ids // classes * per_row + (col_ids // 8)[:, None]
    onehot = (
        targets.reshape(-1)[None, :] == jnp.arange(slot_count, dtype=jnp.int32)[:, None]
    ).astype(jnp.float32)
    sums = jnp.dot(
        onehot,
        received.reshape(n_mem * per_pos, BLK * BLK),
        precision=HI,
        preferred_element_type=jnp.float32,
    )
    sums = sums.reshape(slot_count, BLK, BLK)
    owned = lax.psum_scatter(sums, "grp", scatter_dimension=0, tiled=True)
    slots = group * owned_count + jnp.arange(owned_count, dtype=jnp.int32)
    tile_rows = slots // per_row * classes + residue
    tile_cols = slots % per_row * 8 + position
    ridge_blocks = jnp.take(ridge.reshape(NB, BLK), tile_rows, axis=0)
    same = (tile_rows == tile_cols).astype(jnp.float32)
    extra = jnp.eye(BLK, dtype=jnp.float32)[None] * ridge_blocks[:, None, :] * same[:, None, None]
    divisor = jnp.float32(row_count * n_grp * n_mem // 16)
    tiles = owned / divisor + extra
    picker = column_picker(0, tile_rows, tile_cols)
    partial_value = jnp.einsum("it,tpq->ipq", picker, tiles, precision=HI)
    column = lax.psum(partial_value, ("grp", "mem"))
    lower_col = panel_solve(column)
    tiles = apply_step(tiles, lower_col, 0, tile_rows, tile_cols)
    return tiles[None]


def on_device_fast(design, active_blocks, ridge):
    n_mem = lax.axis_size("mem")
    n_grp = lax.axis_size("grp")
    member = lax.axis_index("mem")
    group = lax.axis_index("grp")
    per_row = NB // ACT
    sizes = (1, 2, 5)
    starts = (0, 1, 3)
    row_count = design.shape[0]
    divisor = jnp.float32(row_count * n_grp * n_mem // 16)
    eye = jnp.eye(BLK, dtype=jnp.float32)
    ridge_blocks = ridge.reshape(NB, BLK)

    blocks = design.reshape(row_count, ACT, BLK)
    id_rows = jnp.zeros((8, BLK), jnp.float32).at[0, :ACT].set(active_blocks[0].astype(jnp.float32))
    id_rows = jnp.broadcast_to(id_rows[None, None], (n_mem, 1, 8, BLK))
    grp_ids = jnp.arange(n_grp, dtype=jnp.int32)
    q_ids = jnp.arange(per_row, dtype=jnp.int32)

    owned_parts = []
    prev = None
    for k in range(len(sizes)):
        per_chunk = sizes[k]
        lo = starts[k]
        pos_ids = jnp.arange(per_chunk, dtype=jnp.int32)
        piece = jnp.einsum(
            "nak,nbl->bakl", blocks[:, lo:lo + per_chunk], blocks, preferred_element_type=jnp.float32
        )
        if prev is not None:
            piece, prev = lax.optimization_barrier((piece, prev))
        else:
            ids_here = jnp.broadcast_to(id_rows, (n_mem, per_chunk, 8, BLK))
            piece = jnp.concatenate([piece, ids_here], axis=2)
        got_piece = lax.all_to_all(piece, "mem", split_axis=0, concat_axis=0, tiled=True)
        if prev is None:
            everyone = got_piece[:, 0, BLK, :ACT].astype(jnp.int32)
            got_piece = got_piece[:, :, :BLK]
            row_grp = everyone // 8
            col_grp = jnp.take(everyone, member, axis=1) // 8
            zero_on = everyone[:, 0] == 0
        got_piece = got_piece.reshape(n_mem, per_chunk, BLK, BLK)
        prev = got_piece
        rg = row_grp[:, lo:lo + per_chunk]
        sel = (
            (pos_ids[None, :, None, None, None] == pos_ids[None, None, None, None, :])
            & (rg[None, None, None, :, :] == grp_ids[:, None, None, None, None])
            & (col_grp[None, None, None, :, None] == q_ids[None, None, :, None, None])
        )
        sel = sel.reshape(n_grp, per_chunk * per_row, n_mem * per_chunk)
        if k == 0:
            first = pos_ids == 0
            col_sel = (
                (col_grp[None, :, None] == grp_ids[:, None, None])
                & zero_on[None, :, None]
                & first[None, None, :]
            ).reshape(n_grp, 1, n_mem * per_chunk)
            sel = jnp.concatenate([sel, col_sel], axis=1)
        width = sel.shape[1]
        send = jnp.einsum(
            "rs,skl->rkl",
            sel.reshape(n_grp * width, n_mem * per_chunk).astype(jnp.float32),
            got_piece.reshape(n_mem * per_chunk, BLK, BLK),
            precision=lax.Precision.HIGH,
            preferred_element_type=jnp.float32,
        )
        got = lax.psum_scatter(send, "grp", scatter_dimension=0, tiled=True)
        owned_parts.append(got[: per_chunk * per_row])
        if k == 0:
            col_tile = jnp.transpose(got[per_chunk * per_row]) / divisor
    owned = jnp.concatenate(owned_parts, axis=0)

    col_tile, prev = lax.optimization_barrier((col_tile, prev))
    spread = jnp.broadcast_to(col_tile[None], (n_grp, BLK, BLK))
    col_cols = lax.all_to_all(spread, "grp", split_axis=0, concat_axis=0, tiled=True)
    pair = jnp.broadcast_to(jnp.stack([col_tile, col_cols[0]])[None], (n_mem, 2, BLK, BLK))
    pairs = lax.all_to_all(pair, "mem", split_axis=0, concat_axis=0, tiled=True)
    col_rows = pairs[:, 0]
    a00 = pairs[0, 1] + eye * ridge_blocks[0][None, :]
    chol = jnp.linalg.cholesky(a00)
    chol_inv = lax.linalg.triangular_solve(chol, eye, left_side=True, lower=True)

    t = jnp.arange(ACT * per_row, dtype=jnp.int32)
    tile_rows = group * 8 + t // per_row
    tile_cols = (t % per_row) * 8 + member
    same = (tile_rows == tile_cols).astype(jnp.float32)
    diag = eye[None] * jnp.take(ridge_blocks, tile_rows, axis=0)[:, None, :] * same[:, None, None]

    p_rows = jnp.einsum("ipr,qr->ipq", col_rows, chol_inv, precision=HI)
    p_cols = jnp.einsum("ipr,qr->ipq", col_cols, chol_inv, precision=HI)
    row_ids = group * 8 + jnp.arange(8, dtype=jnp.int32)
    col_ids = jnp.arange(per_row, dtype=jnp.int32) * 8 + member
    p_rows = jnp.where((row_ids == 0)[:, None, None], chol[None], p_rows)
    p_cols = jnp.where((col_ids == 0)[:, None, None], chol[None], p_cols)

    update = jnp.einsum("apr,qsr->aqps", p_rows, p_cols, precision=HI)
    update = update.reshape(ACT * per_row, BLK, BLK)
    left_tiles = jnp.repeat(p_rows, per_row, axis=0)
    right_tiles = jnp.tile(p_cols, (ACT, 1, 1))
    trailing = ((tile_rows > 0) & (tile_cols > 0))[:, None, None]
    on_column = (tile_cols == 0)[:, None, None]
    on_row = ((tile_rows == 0) & (tile_cols > 0))[:, None, None]
    addend = jnp.where(trailing, diag - update, diag)
    replaced = on_column | on_row
    override = jnp.where(on_column, left_tiles, jnp.transpose(right_tiles, (0, 2, 1)))
    addend, override = lax.optimization_barrier((addend, override))
    tiles = jnp.where(replaced, override, owned / divisor + addend)
    return tiles[None]


def solution(mesh):
    n_mem = mesh.shape["mem"]
    n_grp = mesh.shape["grp"]
    fast = n_mem == 8 and n_grp * 8 == NB
    body = on_device_fast if fast else on_device_general
    in_specs = (P(("grp", "mem"), None), P(("grp", "mem"), None), P())
    out_specs = P("mem", "grp", None, None)
    return jax.shard_map(
        body, mesh=mesh, in_specs=in_specs, out_specs=out_specs, check_vma=False
    )
```
